32 devices in a mesh: freq: 4 (over z), blk: 8 (over y, x, core).
Axes of the slice: x: 2, y: 2, z: 4, core: 2. Of those that a mesh axis runs over, the one named last changes fastest.
Arguments:
- spectra: bfloat16 [8, 512, 2, 32, 128], P('blk', 'freq'), may hold values from -6 to 6
- pair_offsets: int32 [8, 5], P('blk'), may hold values from 0 to 4, as said below
- pair_count: int32 [8], P('blk'), may hold values from 1 to 5, as said below
Outputs:
- correlations: bfloat16 [8, 5, 128, 256, 128], P('blk', None, 'freq')
The draws below stay inside these ranges and needn't reach their ends.
Inputs may be any that keep to these rules, and one draw needn't show every extreme that they name: `pair_offsets`: for every block, slot 0 holds 0 (the block with itself) and slots 1 to 4 hold the offsets 1 to 4, each once, in an order drawn for each block. `pair_count`: slots at or beyond a block's count are unused; block 0 lists every slot.
All inputs are finite; a program needn't handle non-finite values.
Results may differ from the reference program's by a relative error of at most 0.0052.
Values may be sent and summed in bfloat16 or wider, within the bound.
No kernel may reach another device: no remote copies, remote signals or barrier semaphores. Data moves between devices by JAX's collectives and lax.ppermute only.
A program may use at most 192 MiB of HBM per device.

```python
import math
import jax
import jax.numpy as jnp
from jax import lax

S = 128
F = 512
LAGS = 256
W = 32
REACH = 4
SLOTS = 5
BLOCKS = 8


def draw_pair_count(key, part):
    counts = jax.random.randint(jax.random.fold_in(key, 11), (BLOCKS,), 1, SLOTS + 1)
    chosen = jax.random.randint(jax.random.fold_in(key, 12), (), 0, BLOCKS)
    positions = jnp.arange(BLOCKS)
    full = jnp.logical_or(positions == chosen, positions == 0)
    return jnp.where(full, SLOTS, counts).astype(jnp.int32)


def draw_pair_offsets(key, part):
    scores = jax.random.randint(jax.random.fold_in(key, 21), (BLOCKS, REACH), 0, 2 ** 20) * REACH + jnp.arange(REACH, dtype=jnp.int32)[None, :]
    ordering = jnp.argsort(scores, axis=1).astype(jnp.int32) + 1
    zeros_column = jnp.zeros((BLOCKS, 1), jnp.int32)
    return jnp.concatenate([zeros_column, ordering], axis=1).astype(jnp.int32)


def steps_of(stream_key, extent, cuts, least, top_value):
    gain = 1.0
    for position, parts in cuts:
        steps = jax.random.uniform(jax.random.fold_in(jax.random.fold_in(stream_key, 6), position), (parts,), jnp.float32, least / len(cuts), top_value / len(cuts))
        gain = gain * jnp.repeat(jnp.exp(steps), extent[position] // parts).reshape((-1,) + (1,) * (len(extent) - 1 - position))
    return gain


def gaussian(key, dims, deviation, bound, cuts=(), held_as=jnp.bfloat16):
    loudness = steps_of(key, dims, cuts, -0.22, 0.18) if cuts else 1.0
    entries = jax.random.normal(key, dims, jnp.float32) * deviation * loudness
    return jnp.minimum(jnp.maximum(entries, -bound), bound).astype(held_as)


def setup_inputs(seed: int = 0) -> dict:
    splits = jax.random.split(jax.random.key(seed), 4)
    return {
        "spectra": gaussian(splits[0], (BLOCKS, F, 2, W, S), 1.0, 6.0, ((0, 8), (1, 4))),
        "pair_offsets": draw_pair_offsets(jax.random.fold_in(splits[3], 71), 0),
        "pair_count": draw_pair_count(jax.random.fold_in(splits[3], 71), 0),
    }


def lag_table():
    shifted = jnp.arange(LAGS, dtype=jnp.int32) - LAGS // 2
    bins = jnp.arange(F, dtype=jnp.int32) + 1
    phase = jnp.mod(shifted[:, None] * bins[None, :], 2 * F).astype(jnp.float32) * (jnp.pi / F)
    return jnp.stack([jnp.cos(phase), -jnp.sin(phase)], axis=-1).astype(jnp.bfloat16)

def cross_spectrum(home_spec, partner):
    freq_count, parts_count, windows, stations = home_spec.shape
    row_matrix = home_spec.reshape(freq_count, 2 * windows, stations).astype(jnp.float32)
    real_part = partner[:, 0].astype(jnp.float32)
    imag_part = partner[:, 1].astype(jnp.float32)
    real_rows = jnp.concatenate([real_part, imag_part], axis=1)
    imag_rows = jnp.concatenate([imag_part, -real_part], axis=1)
    column_matrix = jnp.concatenate([real_rows, imag_rows], axis=2)
    return jnp.einsum('fks,fkt->fst', row_matrix, column_matrix) / windows

def lag_transform(crosses, lag_weights):
    count_slots, freq_count, stations, double_width = crosses.shape
    regrouped = crosses.reshape(count_slots, freq_count, stations, 2, double_width // 2)
    lagged = jnp.einsum('lfr,nfsrt->nslt', lag_weights.astype(jnp.float32), regrouped.astype(jnp.float32))
    return (lagged * math.sqrt(2.0 / freq_count)).astype(jnp.bfloat16)

def reference(spectra, pair_offsets, pair_count):
    lag_weights = lag_table()

    def one_block(block_index):
        home_spec = spectra[block_index]

        def one_slot(slot_index):
            partner = spectra[jnp.mod(block_index + pair_offsets[block_index, slot_index], BLOCKS)]
            cross_term = cross_spectrum(home_spec, partner)
            is_live = slot_index < pair_count[block_index]
            return jnp.where(is_live, cross_term, 0.0).astype(jnp.bfloat16)
        crosses = lax.map(one_slot, jnp.arange(SLOTS, dtype=jnp.int32))
        return lag_transform(crosses, lag_weights)
    return lax.map(one_block, jnp.arange(BLOCKS, dtype=jnp.int32))
```

```python
import math

import jax
import jax.numpy as jnp
from jax import lax
from jax.sharding import PartitionSpec as P

F = 512
LAGS = 256
REACH = 4
SLOTS = 5


def from_behind(shard, axis, by):
    size = lax.axis_size(axis)
    return lax.ppermute(shard, axis, [(i, (i + by) % size) for i in range(size)])


def swap(shard, axis, mask):
    size = lax.axis_size(axis)
    return lax.ppermute(shard, axis, [(i, i ^ mask) for i in range(size)])


def lag_table():
    shifted = jnp.arange(LAGS, dtype=jnp.int32) - LAGS // 2
    bins = jnp.arange(F, dtype=jnp.int32) + 1
    phase = jnp.mod(shifted[:, None] * bins[None, :], 2 * F).astype(jnp.float32) * (jnp.pi / F)
    return jnp.stack([jnp.cos(phase), -jnp.sin(phase)], axis=-1).astype(jnp.bfloat16)


def cross_spectrum(home_spec, partner):
    freq_count, parts_count, windows, stations = home_spec.shape
    row_matrix = home_spec.reshape(freq_count, 2 * windows, stations)
    real_part = partner[:, 0]
    imag_part = partner[:, 1]
    real_rows = jnp.concatenate([real_part, imag_part], axis=1)
    imag_rows = jnp.concatenate([imag_part, -real_part], axis=1)
    column_matrix = jnp.concatenate([real_rows, imag_rows], axis=2)
    summed = jnp.einsum(
        "fks,fkt->fst", row_matrix, column_matrix, preferred_element_type=jnp.float32
    )
    return summed / windows


def partner_blocks(own, staged):
    if not staged:
        return [own] + [from_behind(own, "blk", -o) for o in range(1, REACH + 1)]
    b = lax.axis_index("blk")
    x_bit = (b // 2) % 2
    core = b % 2
    r4 = swap(own, "blk", 4)
    r2 = swap(jnp.where(x_bit == 1, own, r4), "blk", 2)
    r1 = swap(jnp.where(core == 1, own, r2), "blk", 1)
    r3 = swap(jnp.where(core == 1, r2, r4), "blk", 1)
    return [own, r1, r2, r3, r4]


def local(spectra, pair_offsets, pair_count, staged):
    own_part = spectra[0]
    own = lax.all_gather(own_part, "freq", axis=0, tiled=True)
    freq_total, _, _, stations = own.shape
    parts = lax.axis_size("freq")
    width = stations // parts
    q = lax.axis_index("freq")
    home = lax.dynamic_slice_in_dim(own, q * width, width, axis=3)
    partners = partner_blocks(own, staged)

    offsets = pair_offsets[0]
    listed = pair_count[0]
    lag_weights = lag_table()
    scale = math.sqrt(2.0 / freq_total)
    out = jnp.zeros((SLOTS, width, LAGS, stations), jnp.bfloat16)
    for o in range(REACH + 1):
        slot = jnp.argmax(offsets == o).astype(jnp.int32)
        cross = cross_spectrum(home, partners[o]).astype(jnp.bfloat16)
        regrouped = cross.reshape(freq_total, width, 2, stations)
        lagged = jnp.einsum(
            "lfr,fsrt->slt", lag_weights, regrouped, preferred_element_type=jnp.float32
        )
        result = (lagged * scale).astype(jnp.bfloat16)
        result = jnp.where(slot < listed, result, jnp.zeros_like(result))
        out = lax.dynamic_update_slice(out, result[None], (slot, 0, 0, 0))
    return out[None]


def solution(mesh):
    staged = mesh.shape["blk"] == 8
    placed = (P("blk", "freq", None, None, None), P("blk", None), P("blk"))
    return jax.shard_map(
        lambda s, po, pc: local(s, po, pc, staged),
        mesh=mesh,
        in_specs=placed,
        out_specs=P("blk", None, "freq", None, None),
        check_vma=False,
    )
```

```python
import math

import jax
import jax.numpy as jnp
import numpy as np
from jax import lax
from jax.sharding import PartitionSpec as P

F = 512
LAGS = 256
REACH = 4
SLOTS = 5
CHUNKS = 4


def from_behind(shard, axis, by):
    size = lax.axis_size(axis)
    return lax.ppermute(shard, axis, [(i, (i + by) % size) for i in range(size)])


def swap(shard, axis, mask):
    size = lax.axis_size(axis)
    return lax.ppermute(shard, axis, [(i, i ^ mask) for i in range(size)])


def lag_table(bins_order):
    shifted = jnp.arange(LAGS, dtype=jnp.int32) - LAGS // 2
    bins = jnp.asarray(bins_order, dtype=jnp.int32) + 1
    phase = jnp.mod(shifted[:, None] * bins[None, :], 2 * F).astype(jnp.float32) * (jnp.pi / F)
    return jnp.stack([jnp.cos(phase), -jnp.sin(phase)], axis=-1).astype(jnp.bfloat16)


def home_rows(home):
    real_part = home[:, 0]
    imag_part = home[:, 1]
    real_cols = jnp.concatenate([real_part, imag_part], axis=1)
    imag_cols = jnp.concatenate([-imag_part, real_part], axis=1)
    return jnp.concatenate([real_cols, imag_cols], axis=2)


def cross_spectrum(rows, partner):
    freq_count, parts_count, windows, stations = partner.shape
    width = rows.shape[2] // 2
    columns = partner.reshape(freq_count, parts_count * windows, stations)
    summed = jnp.einsum("fkS,fkt->fSt", rows, columns, preferred_element_type=jnp.float32)
    return (summed / windows).astype(jnp.bfloat16).reshape(freq_count, 2, width, stations)


def partner_blocks(own, staged):
    if not staged:
        return [own] + [from_behind(own, "blk", -o) for o in range(1, REACH + 1)]
    b = lax.axis_index("blk")
    x_bit = (b // 2) % 2
    core = b % 2
    r4 = swap(own, "blk", 4)
    r2 = swap(jnp.where(x_bit == 1, own, r4), "blk", 2)
    r1 = swap(jnp.where(core == 1, own, r2), "blk", 1)
    r3 = swap(jnp.where(core == 1, r2, r4), "blk", 1)
    return [own, r1, r2, r3, r4]


def local(spectra, pair_offsets, pair_count, staged):
    own_part = spectra[0]
    local_freqs, _, _, stations = own_part.shape
    parts = lax.axis_size("freq")
    freq_total = local_freqs * parts
    chunks = CHUNKS if local_freqs % CHUNKS == 0 else 1
    piece = local_freqs // chunks
    width = stations // parts
    q = lax.axis_index("freq")

    order = np.array(
        [qq * local_freqs + j * piece + i for j in range(chunks) for qq in range(parts) for i in range(piece)]
    )
    crosses = [[] for _ in range(REACH + 1)]
    for j in range(chunks):
        own = lax.all_gather(own_part[j * piece:(j + 1) * piece], "freq", axis=0, tiled=True)
        rows = home_rows(lax.dynamic_slice_in_dim(own, q * width, width, axis=3))
        for o, partner in enumerate(partner_blocks(own, staged)):
            crosses[o].append(cross_spectrum(rows, partner))

    offsets = pair_offsets[0]
    listed = pair_count[0]
    lag_weights = lag_table(order)
    scale = math.sqrt(2.0 / freq_total)
    out = jnp.zeros((SLOTS, width, LAGS, stations), jnp.bfloat16)
    for o in range(REACH + 1):
        slot = jnp.argmax(offsets == o).astype(jnp.int32)
        cross = jnp.concatenate(crosses[o], axis=0)
        lagged = jnp.einsum("lfr,frst->slt", lag_weights, cross, preferred_element_type=jnp.float32)
        factor = jnp.where(slot < listed, scale, 0.0).astype(jnp.float32)
        result = (lagged * factor).astype(jnp.bfloat16)
        out = lax.dynamic_update_slice(out, result[None], (slot, 0, 0, 0))
    return out[None]


def solution(mesh):
    staged = mesh.shape["blk"] == 8
    placed = (P("blk", "freq", None, None, None), P("blk", None), P("blk"))
    return jax.shard_map(
        lambda s, po, pc: local(s, po, pc, staged),
        mesh=mesh,
        in_specs=placed,
        out_specs=P("blk", None, "freq", None, None),
        check_vma=False,
    )
```

```python
import math

import jax
import jax.numpy as jnp
import numpy as np
from jax import lax
from jax.sharding import PartitionSpec as P

F = 512
LAGS = 256
REACH = 4
SLOTS = 5
CHUNKS = 4


def from_behind(shard, axis, by):
    size = lax.axis_size(axis)
    return lax.ppermute(shard, axis, [(i, (i + by) % size) for i in range(size)])


def swap(shard, axis, mask):
    size = lax.axis_size(axis)
    return lax.ppermute(shard, axis, [(i, i ^ mask) for i in range(size)])


def lag_table(bins_order):
    shifted = jnp.arange(LAGS, dtype=jnp.int32) - LAGS // 2
    bins = jnp.asarray(bins_order, dtype=jnp.int32) + 1
    phase = jnp.mod(shifted[:, None] * bins[None, :], 2 * F).astype(jnp.float32) * (jnp.pi / F)
    return jnp.stack([jnp.cos(phase), -jnp.sin(phase)], axis=-1).astype(jnp.bfloat16)


def home_rows(home):
    real_part = home[:, 0]
    imag_part = home[:, 1]
    real_cols = jnp.concatenate([real_part, imag_part], axis=1)
    imag_cols = jnp.concatenate([-imag_part, real_part], axis=1)
    return jnp.concatenate([real_cols, imag_cols], axis=2)


def cross_spectrum(rows, partner):
    freq_count, parts_count, windows, stations = partner.shape
    width = rows.shape[2] // 2
    columns = partner.reshape(freq_count, parts_count * windows, stations)
    summed = jnp.einsum("fkS,fkt->fSt", rows, columns, preferred_element_type=jnp.float32)
    return (summed / windows).astype(jnp.bfloat16).reshape(freq_count, 2, width, stations)


def local(spectra, pair_offsets, pair_count, staged):
    own_part = spectra[0]
    local_freqs, _, _, stations = own_part.shape
    parts = lax.axis_size("freq")
    freq_total = local_freqs * parts
    chunks = CHUNKS if local_freqs % CHUNKS == 0 else 1
    piece = local_freqs // chunks
    width = stations // parts
    q = lax.axis_index("freq")
    b = lax.axis_index("blk")
    x_bit = (b // 2) % 2
    core = b % 2

    order = np.array(
        [qq * local_freqs + j * piece + i for j in range(chunks) for qq in range(parts) for i in range(piece)]
    )
    held = {"part/%d" % j: own_part[j * piece:(j + 1) * piece] for j in range(chunks)}
    crosses = {}
    depth = 4 if staged else 1
    for step in range(chunks + depth + 1):
        made = {}
        j = step
        if j < chunks:
            made["own/%d" % j] = lax.all_gather(held["part/%d" % j], "freq", axis=0, tiled=True)
        j = step - 1
        if 0 <= j < chunks:
            own = held["own/%d" % j]
            made["rows/%d" % j] = home_rows(lax.dynamic_slice_in_dim(own, q * width, width, axis=3))
            if staged:
                made["r4/%d" % j] = swap(own, "blk", 4)
            else:
                for o in range(1, REACH + 1):
                    made["r%d/%d" % (o, j)] = from_behind(own, "blk", -o)
        if staged:
            j = step - 2
            if 0 <= j < chunks:
                made["r2/%d" % j] = swap(jnp.where(x_bit == 1, held["own/%d" % j], held["r4/%d" % j]), "blk", 2)
            j = step - 3
            if 0 <= j < chunks:
                made["r1/%d" % j] = swap(jnp.where(core == 1, held["own/%d" % j], held["r2/%d" % j]), "blk", 1)
                made["r3/%d" % j] = swap(jnp.where(core == 1, held["r2/%d" % j], held["r4/%d" % j]), "blk", 1)
        for key in list(held):
            name, j = key.split("/")[0], int(key.split("/")[-1])
            if name in ("own", "r1", "r2", "r3", "r4"):
                o = 0 if name == "own" else int(name[1])
                if "rows/%d" % j in held and (o, j) not in crosses:
                    made["cross%d/%d" % (o, j)] = cross_spectrum(held["rows/%d" % j], held[key])
                    crosses[(o, j)] = True
        keep = dict(held)
        for j in range(chunks):
            if step >= j:
                keep.pop("part/%d" % j, None)
        keep.update(made)
        held = lax.optimization_barrier(keep)

    offsets = pair_offsets[0]
    listed = pair_count[0]
    weights = lag_table(order).reshape(LAGS, freq_total * 2)
    scale = math.sqrt(2.0 / freq_total)
    out = jnp.zeros((SLOTS, width, LAGS, stations), jnp.bfloat16)
    for o in range(REACH + 1):
        slot = jnp.argmax(offsets == o).astype(jnp.int32)
        cross = jnp.concatenate([held["cross%d/%d" % (o, j)] for j in range(chunks)], axis=0)
        cross = cross.reshape(freq_total * 2, width, stations)
        lagged = jnp.einsum("lK,Kst->lst", weights, cross, preferred_element_type=jnp.float32)
        factor = jnp.where(slot < listed, scale, 0.0).astype(jnp.float32)
        result = jnp.transpose((lagged * factor).astype(jnp.bfloat16), (1, 0, 2))
        out = lax.dynamic_update_slice(out, result[None], (slot, 0, 0, 0))
    return out[None]


def solution(mesh):
    staged = mesh.shape["blk"] == 8
    placed = (P("blk", "freq", None, None, None), P("blk", None), P("blk"))
    return jax.shard_map(
        lambda s, po, pc: local(s, po, pc, staged),
        mesh=mesh,
        in_specs=placed,
        out_specs=P("blk", None, "freq", None, None),
        check_vma=False,
    )
```

```python
import math

import jax
import jax.numpy as jnp
import numpy as np
from jax import lax
from jax.sharding import PartitionSpec as P

F = 512
LAGS = 256
REACH = 4
SLOTS = 5
CHUNKS = 4


def from_behind(shard, axis, by):
    size = lax.axis_size(axis)
    return lax.ppermute(shard, axis, [(i, (i + by) % size) for i in range(size)])


def swap(shard, axis, mask):
    size = lax.axis_size(axis)
    return lax.ppermute(shard, axis, [(i, i ^ mask) for i in range(size)])


def lag_table(bins_order):
    shifted = jnp.arange(LAGS, dtype=jnp.int32) - LAGS // 2
    bins = jnp.asarray(bins_order, dtype=jnp.int32) + 1
    phase = jnp.mod(shifted[:, None] * bins[None, :], 2 * F).astype(jnp.float32) * (jnp.pi / F)
    return jnp.stack([jnp.cos(phase), -jnp.sin(phase)], axis=-1).astype(jnp.bfloat16)


def home_rows(own, start, width):
    freq_count, parts_count, windows, stations = own.shape
    flat = own.reshape(freq_count, parts_count * windows, stations)
    picked = lax.dynamic_slice_in_dim(jnp.transpose(flat, (0, 2, 1)), start, width, axis=1)
    turned = jnp.concatenate([-picked[..., windows:], picked[..., :windows]], axis=2)
    return jnp.concatenate([picked, turned], axis=1)


def cross_spectrum(rows_t, partner):
    freq_count, parts_count, windows, stations = partner.shape
    width = rows_t.shape[1] // 2
    columns = partner.reshape(freq_count, parts_count * windows, stations)
    summed = jnp.einsum("fSk,fkt->fSt", rows_t, columns, preferred_element_type=jnp.float32)
    return (summed / windows).astype(jnp.bfloat16).reshape(freq_count, 2, width, stations)


def local(spectra, pair_offsets, pair_count, staged):
    own_part = spectra[0]
    local_freqs, _, _, stations = own_part.shape
    parts = lax.axis_size("freq")
    freq_total = local_freqs * parts
    chunks = CHUNKS if local_freqs % CHUNKS == 0 else 1
    piece = local_freqs // chunks
    width = stations // parts
    q = lax.axis_index("freq")
    b = lax.axis_index("blk")
    x_bit = (b // 2) % 2
    core = b % 2

    order = np.array(
        [qq * local_freqs + j * piece + i for j in range(chunks) for qq in range(parts) for i in range(piece)]
    )
    held = {"part/%d" % j: own_part[j * piece:(j + 1) * piece] for j in range(chunks)}
    crosses = {}
    depth = 4 if staged else 1
    for step in range(chunks + depth + 1):
        made = {}
        j = step
        if j < chunks:
            made["own/%d" % j] = lax.all_gather(held["part/%d" % j], "freq", axis=0, tiled=True)
        j = step - 1
        if 0 <= j < chunks:
            own = held["own/%d" % j]
            made["rows/%d" % j] = home_rows(own, q * width, width)
            if staged:
                made["r4/%d" % j] = swap(own, "blk", 4)
            else:
                for o in range(1, REACH + 1):
                    made["r%d/%d" % (o, j)] = from_behind(own, "blk", -o)
        if staged:
            j = step - 2
            if 0 <= j < chunks:
                made["r2/%d" % j] = swap(jnp.where(x_bit == 1, held["own/%d" % j], held["r4/%d" % j]), "blk", 2)
            j = step - 3
            if 0 <= j < chunks:
                made["r1/%d" % j] = swap(jnp.where(core == 1, held["own/%d" % j], held["r2/%d" % j]), "blk", 1)
                made["r3/%d" % j] = swap(jnp.where(core == 1, held["r2/%d" % j], held["r4/%d" % j]), "blk", 1)
        for key in list(held):
            if "/" not in key:
                continue
            name, j = key.split("/")[0], int(key.split("/")[-1])
            if name in ("own", "r1", "r2", "r3", "r4"):
                o = 0 if name == "own" else int(name[1])
                if "rows/%d" % j in held and (o, j) not in crosses:
                    part = cross_spectrum(held["rows/%d" % j], held[key])
                    name = "cross%d" % o
                    base = made.get(name, held.get(name))
                    if base is None:
                        base = jnp.zeros((freq_total, 2, width, stations), jnp.bfloat16)
                    made[name] = lax.dynamic_update_slice(base, part, (j * piece * parts, 0, 0, 0))
                    crosses[(o, j)] = True
        keep = dict(held)
        for j in range(chunks):
            if step >= j:
                keep.pop("part/%d" % j, None)
        keep.update(made)
        held = lax.optimization_barrier(keep)

    offsets = pair_offsets[0]
    listed = pair_count[0]
    weights = lag_table(order).reshape(LAGS, freq_total * 2)
    scale = math.sqrt(2.0 / freq_total)
    out = jnp.zeros((SLOTS, width, LAGS, stations), jnp.bfloat16)
    for o in range(REACH + 1):
        slot = jnp.argmax(offsets == o).astype(jnp.int32)
        cross = held["cross%d" % o].reshape(freq_total * 2, width, stations)
        lagged = jnp.einsum("lK,Kst->lst", weights, cross, preferred_element_type=jnp.float32)
        factor = jnp.where(slot < listed, scale, 0.0).astype(jnp.float32)
        result = jnp.transpose((lagged * factor).astype(jnp.bfloat16), (1, 0, 2))
        out = lax.dynamic_update_slice(out, result[None], (slot, 0, 0, 0))
    return out[None]


def solution(mesh):
    staged = mesh.shape["blk"] == 8
    placed = (P("blk", "freq", None, None, None), P("blk", None), P("blk"))
    return jax.shard_map(
        lambda s, po, pc: local(s, po, pc, staged),
        mesh=mesh,
        in_specs=placed,
        out_specs=P("blk", None, "freq", None, None),
        check_vma=False,
    )
```

```python
import math

import jax
import jax.numpy as jnp
import numpy as np
from jax import lax
from jax.sharding import PartitionSpec as P

F = 512
LAGS = 256
REACH = 4
SLOTS = 5
CHUNKS = 8


def from_behind(shard, axis, by):
    size = lax.axis_size(axis)
    return lax.ppermute(shard, axis, [(i, (i + by) % size) for i in range(size)])


def swap(shard, axis, mask):
    size = lax.axis_size(axis)
    return lax.ppermute(shard, axis, [(i, i ^ mask) for i in range(size)])


def lag_table(bins_order):
    shifted = jnp.arange(LAGS, dtype=jnp.int32) - LAGS // 2
    bins = jnp.asarray(bins_order, dtype=jnp.int32) + 1
    phase = jnp.mod(shifted[:, None] * bins[None, :], 2 * F).astype(jnp.float32) * (jnp.pi / F)
    return jnp.stack([jnp.cos(phase), -jnp.sin(phase)], axis=-1).astype(jnp.bfloat16)


def home_rows(own, start, width):
    freq_count, parts_count, windows, stations = own.shape
    flat = own.reshape(freq_count, parts_count * windows, stations)
    picked = lax.dynamic_slice_in_dim(jnp.transpose(flat, (0, 2, 1)), start, width, axis=1)
    turned = jnp.concatenate([-picked[..., windows:], picked[..., :windows]], axis=2)
    return jnp.concatenate([picked, turned], axis=1)


def cross_spectrum(rows_t, partner):
    freq_count, parts_count, windows, stations = partner.shape
    width = rows_t.shape[1] // 2
    columns = partner.reshape(freq_count, parts_count * windows, stations)
    summed = jnp.einsum("fSk,fkt->fSt", rows_t, columns, preferred_element_type=jnp.float32)
    return (summed / windows).astype(jnp.bfloat16).reshape(freq_count, 2, width, stations)


def local(spectra, pair_offsets, pair_count, staged):
    own_part = spectra[0]
    local_freqs, _, _, stations = own_part.shape
    parts = lax.axis_size("freq")
    freq_total = local_freqs * parts
    chunks = CHUNKS if local_freqs % CHUNKS == 0 else 1
    piece = local_freqs // chunks
    width = stations // parts
    q = lax.axis_index("freq")
    b = lax.axis_index("blk")
    x_bit = (b // 2) % 2
    core = b % 2

    order = np.array(
        [qq * local_freqs + j * piece + i for j in range(chunks) for qq in range(parts) for i in range(piece)]
    )
    held = {"part/%d" % j: own_part[j * piece:(j + 1) * piece] for j in range(chunks)}
    crosses = {}
    depth = 4 if staged else 1
    for step in range(chunks + depth + 1):
        made = {}
        j = step
        if j < chunks:
            made["own/%d" % j] = lax.all_gather(held["part/%d" % j], "freq", axis=0, tiled=True)
        j = step - 1
        if 0 <= j < chunks:
            own = held["own/%d" % j]
            made["rows/%d" % j] = home_rows(own, q * width, width)
            if staged:
                made["r4/%d" % j] = swap(own, "blk", 4)
            else:
                for o in range(1, REACH + 1):
                    made["r%d/%d" % (o, j)] = from_behind(own, "blk", -o)
        if staged:
            j = step - 2
            if 0 <= j < chunks:
                made["r2/%d" % j] = swap(jnp.where(x_bit == 1, held["own/%d" % j], held["r4/%d" % j]), "blk", 2)
            j = step - 3
            if 0 <= j < chunks:
                made["r1/%d" % j] = swap(jnp.where(core == 1, held["own/%d" % j], held["r2/%d" % j]), "blk", 1)
                made["r3/%d" % j] = swap(jnp.where(core == 1, held["r2/%d" % j], held["r4/%d" % j]), "blk", 1)
        for key in list(held):
            if "/" not in key:
                continue
            name, j = key.split("/")[0], int(key.split("/")[-1])
            if name in ("own", "r1", "r2", "r3", "r4"):
                o = 0 if name == "own" else int(name[1])
                if "rows/%d" % j in held and (o, j) not in crosses:
                    part = cross_spectrum(held["rows/%d" % j], held[key])
                    name = "cross%d" % o
                    base = made.get(name, held.get(name))
                    if base is None:
                        base = jnp.zeros((freq_total, 2, width, stations), jnp.bfloat16)
                    made[name] = lax.dynamic_update_slice(base, part, (j * piece * parts, 0, 0, 0))
                    crosses[(o, j)] = True
        keep = dict(held)
        for j in range(chunks):
            if step >= j:
                keep.pop("part/%d" % j, None)
        keep.update(made)
        held = lax.optimization_barrier(keep)

    offsets = pair_offsets[0]
    listed = pair_count[0]
    weights = lag_table(order).reshape(LAGS, freq_total * 2)
    scale = math.sqrt(2.0 / freq_total)
    out = jnp.zeros((SLOTS, width, LAGS, stations), jnp.bfloat16)
    for o in range(REACH + 1):
        slot = jnp.argmax(offsets == o).astype(jnp.int32)
        cross = held["cross%d" % o].reshape(freq_total * 2, width, stations)
        lagged = jnp.einsum("lK,Kst->lst", weights, cross, preferred_element_type=jnp.float32)
        factor = jnp.where(slot < listed, scale, 0.0).astype(jnp.float32)
        result = jnp.transpose((lagged * factor).astype(jnp.bfloat16), (1, 0, 2))
        out = lax.dynamic_update_slice(out, result[None], (slot, 0, 0, 0))
    return out[None]


def solution(mesh):
    staged = mesh.shape["blk"] == 8
    placed = (P("blk", "freq", None, None, None), P("blk", None), P("blk"))
    return jax.shard_map(
        lambda s, po, pc: local(s, po, pc, staged),
        mesh=mesh,
        in_specs=placed,
        out_specs=P("blk", None, "freq", None, None),
        check_vma=False,
    )
```

```python
import math

import jax
import jax.numpy as jnp
import numpy as np
from jax import lax
from jax.sharding import PartitionSpec as P

F = 512
LAGS = 256
REACH = 4
SLOTS = 5
CHUNKS = 8


def from_behind(shard, axis, by):
    size = lax.axis_size(axis)
    return lax.ppermute(shard, axis, [(i, (i + by) % size) for i in range(size)])


def swap(shard, axis, mask):
    size = lax.axis_size(axis)
    return lax.ppermute(shard, axis, [(i, i ^ mask) for i in range(size)])


def lag_table(bins_order):
    shifted = jnp.arange(LAGS, dtype=jnp.int32) - LAGS // 2
    bins = jnp.asarray(bins_order, dtype=jnp.int32) + 1
    phase = jnp.mod(shifted[:, None] * bins[None, :], 2 * F).astype(jnp.float32) * (jnp.pi / F)
    return jnp.stack([jnp.cos(phase), -jnp.sin(phase)], axis=-1).astype(jnp.bfloat16)


def home_rows(own, start, width):
    freq_count, parts_count, windows, stations = own.shape
    flat = own.reshape(freq_count, parts_count * windows, stations)
    picked = lax.dynamic_slice_in_dim(jnp.transpose(flat, (0, 2, 1)), start, width, axis=1)
    turned = jnp.concatenate([-picked[..., windows:], picked[..., :windows]], axis=2)
    return jnp.concatenate([picked, turned], axis=1)


def cross_spectrum(rows_t, partner):
    freq_count, parts_count, windows, stations = partner.shape
    width = rows_t.shape[1] // 2
    columns = partner.reshape(freq_count, parts_count * windows, stations)
    summed = jnp.einsum("fSk,fkt->fSt", rows_t, columns, preferred_element_type=jnp.float32)
    return (summed / windows).astype(jnp.bfloat16).reshape(freq_count, 2, width, stations)


def local(spectra, pair_offsets, pair_count, staged):
    own_part = spectra[0]
    local_freqs, _, _, stations = own_part.shape
    parts = lax.axis_size("freq")
    freq_total = local_freqs * parts
    chunks = CHUNKS if local_freqs % CHUNKS == 0 else 1
    piece = local_freqs // chunks
    width = stations // parts
    q = lax.axis_index("freq")
    b = lax.axis_index("blk")
    x_bit = (b // 2) % 2
    core = b % 2

    order = np.array(
        [qq * local_freqs + j * piece + i for j in range(chunks) for qq in range(parts) for i in range(piece)]
    )
    held = {"part/%d" % j: own_part[j * piece:(j + 1) * piece] for j in range(chunks)}
    crosses = {}
    depth = 4 if staged else 1
    for step in range(chunks + depth + 1):
        made = {}
        if step == 0:
            for o in range(REACH + 1):
                made["cross%d" % o] = jnp.zeros((freq_total, 2, width, stations), jnp.bfloat16)
            made["out"] = jnp.zeros((SLOTS, width, LAGS, stations), jnp.bfloat16)
            made["weights"] = lag_table(order).reshape(LAGS, freq_total * 2)
        j = step
        if j < chunks:
            made["own/%d" % j] = lax.all_gather(held["part/%d" % j], "freq", axis=0, tiled=True)
        j = step - 1
        if 0 <= j < chunks:
            own = held["own/%d" % j]
            made["rows/%d" % j] = home_rows(own, q * width, width)
            if staged:
                made["r4/%d" % j] = swap(own, "blk", 4)
            else:
                for o in range(1, REACH + 1):
                    made["r%d/%d" % (o, j)] = from_behind(own, "blk", -o)
        if staged:
            j = step - 2
            if 0 <= j < chunks:
                made["r2/%d" % j] = swap(jnp.where(x_bit == 1, held["own/%d" % j], held["r4/%d" % j]), "blk", 2)
            j = step - 3
            if 0 <= j < chunks:
                made["r1/%d" % j] = swap(jnp.where(core == 1, held["own/%d" % j], held["r2/%d" % j]), "blk", 1)
                made["r3/%d" % j] = swap(jnp.where(core == 1, held["r2/%d" % j], held["r4/%d" % j]), "blk", 1)
        for key in list(held):
            if "/" not in key:
                continue
            name, j = key.split("/")[0], int(key.split("/")[-1])
            if name in ("own", "r1", "r2", "r3", "r4"):
                o = 0 if name == "own" else int(name[1])
                if "rows/%d" % j in held and (o, j) not in crosses:
                    part = cross_spectrum(held["rows/%d" % j], held[key])
                    name = "cross%d" % o
                    base = made.get(name, held.get(name))
                    made[name] = lax.dynamic_update_slice(base, part, (j * piece * parts, 0, 0, 0))
                    crosses[(o, j)] = True
        keep = dict(held)
        for j in range(chunks):
            if step >= j:
                keep.pop("part/%d" % j, None)
        keep.update(made)
        held = lax.optimization_barrier(keep)

    offsets = pair_offsets[0]
    listed = pair_count[0]
    weights = held["weights"]
    scale = math.sqrt(2.0 / freq_total)
    out = held["out"]
    for o in range(REACH + 1):
        slot = jnp.argmax(offsets == o).astype(jnp.int32)
        cross = held["cross%d" % o].reshape(freq_total * 2, width, stations)
        lagged = jnp.einsum("lK,Kst->lst", weights, cross, preferred_element_type=jnp.float32)
        factor = jnp.where(slot < listed, scale, 0.0).astype(jnp.float32)
        result = jnp.transpose((lagged * factor).astype(jnp.bfloat16), (1, 0, 2))
        out = lax.dynamic_update_slice(out, result[None], (slot, 0, 0, 0))
    return out[None]


def solution(mesh):
    staged = mesh.shape["blk"] == 8
    placed = (P("blk", "freq", None, None, None), P("blk", None), P("blk"))
    return jax.shard_map(
        lambda s, po, pc: local(s, po, pc, staged),
        mesh=mesh,
        in_specs=placed,
        out_specs=P("blk", None, "freq", None, None),
        check_vma=False,
    )
```

```python
import math

import jax
import jax.numpy as jnp
import numpy as np
from jax import lax
from jax.sharding import PartitionSpec as P

F = 512
LAGS = 256
REACH = 4
SLOTS = 5
CHUNKS = 8


def from_behind(shard, axis, by):
    size = lax.axis_size(axis)
    return lax.ppermute(shard, axis, [(i, (i + by) % size) for i in range(size)])


def swap(shard, axis, mask):
    size = lax.axis_size(axis)
    return lax.ppermute(shard, axis, [(i, i ^ mask) for i in range(size)])


def lag_table(bins_order):
    shifted = jnp.arange(LAGS, dtype=jnp.int32) - LAGS // 2
    bins = jnp.asarray(bins_order, dtype=jnp.int32) + 1
    phase = jnp.mod(shifted[:, None] * bins[None, :], 2 * F).astype(jnp.float32) * (jnp.pi / F)
    return jnp.stack([jnp.cos(phase), -jnp.sin(phase)], axis=-1).astype(jnp.bfloat16)


def home_rows(own, start, width):
    freq_count, parts_count, windows, stations = own.shape
    flat = own.reshape(freq_count, parts_count * windows, stations)
    picked = lax.dynamic_slice_in_dim(jnp.transpose(flat, (0, 2, 1)), start, width, axis=1)
    turned = jnp.concatenate([-picked[..., windows:], picked[..., :windows]], axis=2)
    return jnp.concatenate([picked, turned], axis=1)


def cross_spectrum(rows_t, partner):
    freq_count, parts_count, windows, stations = partner.shape
    width = rows_t.shape[1] // 2
    columns = partner.reshape(freq_count, parts_count * windows, stations)
    summed = jnp.einsum("fSk,fkt->fSt", rows_t, columns, preferred_element_type=jnp.float32)
    return (summed / windows).astype(jnp.bfloat16).reshape(freq_count, 2, width, stations)


def local(spectra, pair_offsets, pair_count, staged):
    own_part = spectra[0]
    local_freqs, _, _, stations = own_part.shape
    parts = lax.axis_size("freq")
    freq_total = local_freqs * parts
    chunks = CHUNKS if local_freqs % CHUNKS == 0 else 1
    piece = local_freqs // chunks
    width = stations // parts
    q = lax.axis_index("freq")
    b = lax.axis_index("blk")
    x_bit = (b // 2) % 2
    core = b % 2

    order = np.array(
        [qq * local_freqs + j * piece + i for j in range(chunks) for qq in range(parts) for i in range(piece)]
    )
    held = {"part/%d" % j: own_part[j * piece:(j + 1) * piece] for j in range(chunks)}
    crosses = {}
    depth = 4 if staged else 1
    for step in range(chunks + depth + 1):
        made = {}
        j = step
        if j < chunks:
            made["own/%d" % j] = lax.all_gather(held["part/%d" % j], "freq", axis=0, tiled=True)
        j = step - 1
        if 0 <= j < chunks:
            own = held["own/%d" % j]
            made["rows/%d" % j] = home_rows(own, q * width, width)
            if staged:
                made["r4/%d" % j] = swap(own, "blk", 4)
            else:
                for o in range(1, REACH + 1):
                    made["r%d/%d" % (o, j)] = from_behind(own, "blk", -o)
        if staged:
            j = step - 2
            if 0 <= j < chunks:
                made["r2/%d" % j] = swap(jnp.where(x_bit == 1, held["own/%d" % j], held["r4/%d" % j]), "blk", 2)
            j = step - 3
            if 0 <= j < chunks:
                made["r1/%d" % j] = swap(jnp.where(core == 1, held["own/%d" % j], held["r2/%d" % j]), "blk", 1)
                made["r3/%d" % j] = swap(jnp.where(core == 1, held["r2/%d" % j], held["r4/%d" % j]), "blk", 1)
        for key in list(held):
            if "/" not in key:
                continue
            name, j = key.split("/")[0], int(key.split("/")[-1])
            if name in ("own", "r1", "r2", "r3", "r4"):
                o = 0 if name == "own" else int(name[1])
                if "rows/%d" % j in held and (o, j) not in crosses:
                    part = cross_spectrum(held["rows/%d" % j], held[key])
                    name = "cross%d" % o
                    base = made.get(name, held.get(name))
                    if base is None:
                        base = jnp.zeros((freq_total, 2, width, stations), jnp.bfloat16)
                    made[name] = lax.dynamic_update_slice(base, part, (j * piece * parts, 0, 0, 0))
                    crosses[(o, j)] = True
        keep = dict(held)
        for j in range(chunks):
            if step >= j:
                keep.pop("part/%d" % j, None)
            if all((o, j) in crosses for o in range(REACH + 1)):
                for name in ("own", "rows", "r1", "r2", "r3", "r4"):
                    keep.pop("%s/%d" % (name, j), None)
        keep.update(made)
        held = lax.optimization_barrier(keep)

    offsets = pair_offsets[0]
    listed = pair_count[0]
    weights = lag_table(order).reshape(LAGS, freq_total * 2)
    scale = math.sqrt(2.0 / freq_total)
    out = jnp.zeros((SLOTS, width, LAGS, stations), jnp.bfloat16)
    for o in range(REACH + 1):
        slot = jnp.argmax(offsets == o).astype(jnp.int32)
        cross = held["cross%d" % o].reshape(freq_total * 2, width, stations)
        lagged = jnp.einsum("lK,Kst->lst", weights, cross, preferred_element_type=jnp.float32)
        factor = jnp.where(slot < listed, scale, 0.0).astype(jnp.float32)
        result = jnp.transpose((lagged * factor).astype(jnp.bfloat16), (1, 0, 2))
        out = lax.dynamic_update_slice(out, result[None], (slot, 0, 0, 0))
    return out[None]


def solution(mesh):
    staged = mesh.shape["blk"] == 8
    placed = (P("blk", "freq", None, None, None), P("blk", None), P("blk"))
    return jax.shard_map(
        lambda s, po, pc: local(s, po, pc, staged),
        mesh=mesh,
        in_specs=placed,
        out_specs=P("blk", None, "freq", None, None),
        check_vma=False,
    )
```

```python
import math

import jax
import jax.numpy as jnp
import numpy as np
from jax import lax
from jax.sharding import PartitionSpec as P

F = 512
LAGS = 256
REACH = 4
SLOTS = 5
CHUNKS = 8


def from_behind(shard, axis, by):
    size = lax.axis_size(axis)
    return lax.ppermute(shard, axis, [(i, (i + by) % size) for i in range(size)])


def swap(shard, axis, mask):
    size = lax.axis_size(axis)
    return lax.ppermute(shard, axis, [(i, i ^ mask) for i in range(size)])


def lag_table(bins_order):
    shifted = jnp.arange(LAGS, dtype=jnp.int32) - LAGS // 2
    bins = jnp.asarray(bins_order, dtype=jnp.int32) + 1
    phase = jnp.mod(shifted[:, None] * bins[None, :], 2 * F).astype(jnp.float32) * (jnp.pi / F)
    return jnp.stack([jnp.cos(phase), -jnp.sin(phase)], axis=-1).astype(jnp.bfloat16)


def home_rows(own, start, width):
    freq_count, parts_count, windows, stations = own.shape
    flat = own.reshape(freq_count, parts_count * windows, stations)
    picked = lax.dynamic_slice_in_dim(jnp.transpose(flat, (0, 2, 1)), start, width, axis=1)
    turned = jnp.concatenate([-picked[..., windows:], picked[..., :windows]], axis=2)
    return jnp.concatenate([picked, turned], axis=1)


def cross_spectrum(rows_t, partner):
    freq_count, parts_count, windows, stations = partner.shape
    width = rows_t.shape[1] // 2
    columns = partner.reshape(freq_count, parts_count * windows, stations)
    summed = jnp.einsum("fSk,fkt->fSt", rows_t, columns, preferred_element_type=jnp.float32)
    return (summed / windows).astype(jnp.bfloat16).reshape(freq_count, 2, width, stations)


def local(spectra, pair_offsets, pair_count, staged):
    own_part = spectra[0]
    local_freqs, _, _, stations = own_part.shape
    parts = lax.axis_size("freq")
    freq_total = local_freqs * parts
    chunks = CHUNKS if local_freqs % CHUNKS == 0 else 1
    piece = local_freqs // chunks
    width = stations // parts
    q = lax.axis_index("freq")
    b = lax.axis_index("blk")
    x_bit = (b // 2) % 2
    core = b % 2

    order = np.array(
        [qq * local_freqs + j * piece + i for j in range(chunks) for qq in range(parts) for i in range(piece)]
    )
    held = {"part/%d" % j: own_part[j * piece:(j + 1) * piece] for j in range(chunks)}
    crosses = {}
    depth = 4 if staged else 1
    for step in range(chunks + depth + 1):
        made = {}
        if step == 0:
            made["weights"] = lag_table(order).reshape(LAGS, freq_total * 2)
        j = step
        if j < chunks:
            made["own/%d" % j] = lax.all_gather(held["part/%d" % j], "freq", axis=0, tiled=True)
        j = step - 1
        if 0 <= j < chunks:
            own = held["own/%d" % j]
            made["rows/%d" % j] = home_rows(own, q * width, width)
            if staged:
                made["r4/%d" % j] = swap(own, "blk", 4)
            else:
                for o in range(1, REACH + 1):
                    made["r%d/%d" % (o, j)] = from_behind(own, "blk", -o)
        if staged:
            j = step - 2
            if 0 <= j < chunks:
                made["r2/%d" % j] = swap(jnp.where(x_bit == 1, held["own/%d" % j], held["r4/%d" % j]), "blk", 2)
            j = step - 3
            if 0 <= j < chunks:
                own, r2, r4 = held["own/%d" % j], held["r2/%d" % j], held["r4/%d" % j]
                both = swap(jnp.where(core == 1, jnp.stack([own, r2]), jnp.stack([r2, r4])), "blk", 1)
                made["r1/%d" % j] = both[0]
                made["r3/%d" % j] = both[1]
        for key in list(held):
            if "/" not in key:
                continue
            name, j = key.split("/")[0], int(key.split("/")[-1])
            if name in ("own", "r1", "r2", "r3", "r4"):
                o = 0 if name == "own" else int(name[1])
                if "rows/%d" % j in held and (o, j) not in crosses:
                    part = cross_spectrum(held["rows/%d" % j], held[key])
                    name = "cross%d" % o
                    base = made.get(name, held.get(name))
                    if base is None:
                        base = jnp.zeros((freq_total, 2, width, stations), jnp.bfloat16)
                    made[name] = lax.dynamic_update_slice(base, part, (j * piece * parts, 0, 0, 0))
                    crosses[(o, j)] = True
        keep = dict(held)
        for j in range(chunks):
            if step >= j:
                keep.pop("part/%d" % j, None)
            if all((o, j) in crosses for o in range(REACH + 1)):
                for name in ("own", "rows", "r1", "r2", "r3", "r4"):
                    keep.pop("%s/%d" % (name, j), None)
        keep.update(made)
        held = lax.optimization_barrier(keep)

    offsets = pair_offsets[0]
    listed = pair_count[0]
    weights = held["weights"]
    scale = math.sqrt(2.0 / freq_total)
    out = jnp.zeros((SLOTS, width, LAGS, stations), jnp.bfloat16)
    for o in range(REACH + 1):
        slot = jnp.argmax(offsets == o).astype(jnp.int32)
        cross = held["cross%d" % o].reshape(freq_total * 2, width, stations)
        lagged = jnp.einsum("lK,Kst->lst", weights, cross, preferred_element_type=jnp.float32)
        factor = jnp.where(slot < listed, scale, 0.0).astype(jnp.float32)
        result = jnp.transpose((lagged * factor).astype(jnp.bfloat16), (1, 0, 2))
        out = lax.dynamic_update_slice(out, result[None], (slot, 0, 0, 0))
    return out[None]


def solution(mesh):
    staged = mesh.shape["blk"] == 8
    placed = (P("blk", "freq", None, None, None), P("blk", None), P("blk"))
    return jax.shard_map(
        lambda s, po, pc: local(s, po, pc, staged),
        mesh=mesh,
        in_specs=placed,
        out_specs=P("blk", None, "freq", None, None),
        check_vma=False,
    )
```

```python
import math

import jax
import jax.numpy as jnp
import numpy as np
from jax import lax
from jax.sharding import PartitionSpec as P

F = 512
LAGS = 256
REACH = 4
SLOTS = 5
CHUNKS = 8


def from_behind(shard, axis, by):
    size = lax.axis_size(axis)
    return lax.ppermute(shard, axis, [(i, (i + by) % size) for i in range(size)])


def swap(shard, axis, mask):
    size = lax.axis_size(axis)
    return lax.ppermute(shard, axis, [(i, i ^ mask) for i in range(size)])


def lag_table(bins_order):
    shifted = jnp.arange(LAGS, dtype=jnp.int32) - LAGS // 2
    bins = jnp.asarray(bins_order, dtype=jnp.int32) + 1
    phase = jnp.mod(shifted[:, None] * bins[None, :], 2 * F).astype(jnp.float32) * (jnp.pi / F)
    return jnp.stack([jnp.cos(phase), -jnp.sin(phase)], axis=-1).astype(jnp.bfloat16)


def home_rows(own, start, width):
    freq_count, parts_count, windows, stations = own.shape
    flat = own.reshape(freq_count, parts_count * windows, stations)
    picked = lax.dynamic_slice_in_dim(jnp.transpose(flat, (0, 2, 1)), start, width, axis=1)
    turned = jnp.concatenate([-picked[..., windows:], picked[..., :windows]], axis=2)
    return jnp.concatenate([picked, turned], axis=1)


def cross_spectrum(rows_t, partner):
    freq_count, parts_count, windows, stations = partner.shape
    width = rows_t.shape[1] // 2
    columns = partner.reshape(freq_count, parts_count * windows, stations)
    summed = jnp.einsum("fSk,fkt->fSt", rows_t, columns, preferred_element_type=jnp.float32)
    return (summed / windows).astype(jnp.bfloat16).reshape(freq_count, 2, width, stations)


def local(spectra, pair_offsets, pair_count, staged):
    own_part = spectra[0]
    local_freqs, _, _, stations = own_part.shape
    parts = lax.axis_size("freq")
    freq_total = local_freqs * parts
    chunks = CHUNKS if local_freqs % CHUNKS == 0 else 1
    piece = local_freqs // chunks
    width = stations // parts
    q = lax.axis_index("freq")
    b = lax.axis_index("blk")
    x_bit = (b // 2) % 2
    core = b % 2

    order = np.array(
        [qq * local_freqs + j * piece + i for j in range(chunks) for qq in range(parts) for i in range(piece)]
    )
    held = {"part/%d" % j: own_part[j * piece:(j + 1) * piece] for j in range(chunks)}
    crosses = {}
    depth = 4 if staged else 1
    for step in range(chunks + depth + 1):
        made = {}
        j = step
        if j < chunks:
            made["own/%d" % j] = lax.all_gather(held["part/%d" % j], "freq", axis=0, tiled=True)
        j = step - 1
        if 0 <= j < chunks:
            own = held["own/%d" % j]
            made["rows/%d" % j] = home_rows(own, q * width, width)
            if staged:
                made["r4/%d" % j] = swap(own, "blk", 4)
            else:
                for o in range(1, REACH + 1):
                    made["r%d/%d" % (o, j)] = from_behind(own, "blk", -o)
        if staged:
            j = step - 2
            if 0 <= j < chunks:
                made["r2/%d" % j] = swap(jnp.where(x_bit == 1, held["own/%d" % j], held["r4/%d" % j]), "blk", 2)
            j = step - 3
            if 0 <= j < chunks:
                own, r2, r4 = held["own/%d" % j], held["r2/%d" % j], held["r4/%d" % j]
                both = swap(jnp.where(core == 1, jnp.stack([own, r2]), jnp.stack([r2, r4])), "blk", 1)
                made["r1/%d" % j] = both[0]
                made["r3/%d" % j] = both[1]
        for key in list(held):
            if "/" not in key:
                continue
            name, j = key.split("/")[0], int(key.split("/")[-1])
            if name in ("own", "r1", "r2", "r3", "r4"):
                o = 0 if name == "own" else int(name[1])
                if "rows/%d" % j in held and (o, j) not in crosses:
                    part = cross_spectrum(held["rows/%d" % j], held[key])
                    name = "cross%d" % o
                    base = made.get(name, held.get(name))
                    if base is None:
                        base = jnp.zeros((freq_total, 2, width, stations), jnp.bfloat16)
                    made[name] = lax.dynamic_update_slice(base, part, (j * piece * parts, 0, 0, 0))
                    crosses[(o, j)] = True
        keep = dict(held)
        for j in range(chunks):
            if step >= j:
                keep.pop("part/%d" % j, None)
            if all((o, j) in crosses for o in range(REACH + 1)):
                for name in ("own", "rows", "r1", "r2", "r3", "r4"):
                    keep.pop("%s/%d" % (name, j), None)
        keep.update(made)
        held = lax.optimization_barrier(keep)

    offsets = pair_offsets[0]
    listed = pair_count[0]
    weights = lag_table(order).reshape(LAGS, freq_total * 2)
    scale = math.sqrt(2.0 / freq_total)
    out = jnp.zeros((SLOTS, width, LAGS, stations), jnp.bfloat16)
    for o in range(REACH + 1):
        slot = jnp.argmax(offsets == o).astype(jnp.int32)
        cross = held["cross%d" % o].reshape(freq_total * 2, width, stations)
        lagged = jnp.einsum("lK,Kst->lst", weights, cross, preferred_element_type=jnp.float32)
        factor = jnp.where(slot < listed, scale, 0.0).astype(jnp.float32)
        result = jnp.transpose((lagged * factor).astype(jnp.bfloat16), (1, 0, 2))
        out = lax.dynamic_update_slice(out, result[None], (slot, 0, 0, 0))
    return out[None]


def solution(mesh):
    staged = mesh.shape["blk"] == 8
    placed = (P("blk", "freq", None, None, None), P("blk", None), P("blk"))
    return jax.shard_map(
        lambda s, po, pc: local(s, po, pc, staged),
        mesh=mesh,
        in_specs=placed,
        out_specs=P("blk", None, "freq", None, None),
        check_vma=False,
    )
```

```python
import math

import jax
import jax.numpy as jnp
import numpy as np
from jax import lax
from jax.sharding import PartitionSpec as P

F = 512
LAGS = 256
REACH = 4
SLOTS = 5
CHUNKS = 4


def from_behind(shard, axis, by):
    size = lax.axis_size(axis)
    return lax.ppermute(shard, axis, [(i, (i + by) % size) for i in range(size)])


def swap(shard, axis, mask):
    size = lax.axis_size(axis)
    return lax.ppermute(shard, axis, [(i, i ^ mask) for i in range(size)])


def lag_table(bins_order):
    shifted = jnp.arange(LAGS, dtype=jnp.int32) - LAGS // 2
    bins = jnp.asarray(bins_order, dtype=jnp.int32) + 1
    phase = jnp.mod(shifted[:, None] * bins[None, :], 2 * F).astype(jnp.float32) * (jnp.pi / F)
    return jnp.stack([jnp.cos(phase), -jnp.sin(phase)], axis=-1).astype(jnp.bfloat16)


def home_rows(own, start, width):
    freq_count, parts_count, windows, stations = own.shape
    flat = own.reshape(freq_count, parts_count * windows, stations)
    picked = lax.dynamic_slice_in_dim(jnp.transpose(flat, (0, 2, 1)), start, width, axis=1)
    turned = jnp.concatenate([-picked[..., windows:], picked[..., :windows]], axis=2)
    return jnp.concatenate([picked, turned], axis=1)


def cross_spectrum(rows_t, partner):
    freq_count, parts_count, windows, stations = partner.shape
    width = rows_t.shape[1] // 2
    columns = partner.reshape(freq_count, parts_count * windows, stations)
    summed = jnp.einsum("fSk,fkt->fSt", rows_t, columns, preferred_element_type=jnp.float32)
    return (summed / windows).astype(jnp.bfloat16).reshape(freq_count, 2, width, stations)


def local(spectra, pair_offsets, pair_count, staged):
    own_part = spectra[0]
    local_freqs, _, _, stations = own_part.shape
    parts = lax.axis_size("freq")
    freq_total = local_freqs * parts
    chunks = CHUNKS if local_freqs % CHUNKS == 0 else 1
    piece = local_freqs // chunks
    width = stations // parts
    q = lax.axis_index("freq")
    b = lax.axis_index("blk")
    x_bit = (b // 2) % 2
    core = b % 2

    order = np.array(
        [qq * local_freqs + j * piece + i for j in range(chunks) for qq in range(parts) for i in range(piece)]
    )
    held = {"part/%d" % j: own_part[j * piece:(j + 1) * piece] for j in range(chunks)}
    crosses = {}
    depth = 4 if staged else 1
    for step in range(chunks + depth + 1):
        made = {}
        j = step
        if j < chunks:
            made["own/%d" % j] = lax.all_gather(held["part/%d" % j], "freq", axis=0, tiled=True)
        j = step - 1
        if 0 <= j < chunks:
            own = held["own/%d" % j]
            made["rows/%d" % j] = home_rows(own, q * width, width)
            if staged:
                made["r4/%d" % j] = swap(own, "blk", 4)
            else:
                for o in range(1, REACH + 1):
                    made["r%d/%d" % (o, j)] = from_behind(own, "blk", -o)
        if staged:
            j = step - 2
            if 0 <= j < chunks:
                made["r2/%d" % j] = swap(jnp.where(x_bit == 1, held["own/%d" % j], held["r4/%d" % j]), "blk", 2)
            j = step - 3
            if 0 <= j < chunks:
                made["r1/%d" % j] = swap(jnp.where(core == 1, held["own/%d" % j], held["r2/%d" % j]), "blk", 1)
                made["r3/%d" % j] = swap(jnp.where(core == 1, held["r2/%d" % j], held["r4/%d" % j]), "blk", 1)
        for key in list(held):
            if "/" not in key:
                continue
            name, j = key.split("/")[0], int(key.split("/")[-1])
            if name in ("own", "r1", "r2", "r3", "r4"):
                o = 0 if name == "own" else int(name[1])
                if "rows/%d" % j in held and (o, j) not in crosses:
                    part = cross_spectrum(held["rows/%d" % j], held[key])
                    name = "cross%d" % o
                    base = made.get(name, held.get(name))
                    if base is None:
                        base = jnp.zeros((freq_total, 2, width, stations), jnp.bfloat16)
                    made[name] = lax.dynamic_update_slice(base, part, (j * piece * parts, 0, 0, 0))
                    crosses[(o, j)] = True
        keep = dict(held)
        for j in range(chunks):
            if step >= j:
                keep.pop("part/%d" % j, None)
            if all((o, j) in crosses for o in range(REACH + 1)):
                for name in ("own", "rows", "r1", "r2", "r3", "r4"):
                    keep.pop("%s/%d" % (name, j), None)
        keep.update(made)
        held = lax.optimization_barrier(keep)

    offsets = pair_offsets[0]
    listed = pair_count[0]
    weights = lag_table(order).reshape(LAGS, freq_total * 2)
    scale = math.sqrt(2.0 / freq_total)
    out = jnp.zeros((SLOTS, width, LAGS, stations), jnp.bfloat16)
    for o in range(REACH + 1):
        slot = jnp.argmax(offsets == o).astype(jnp.int32)
        cross = held["cross%d" % o].reshape(freq_total * 2, width, stations)
        lagged = jnp.einsum("lK,Kst->lst", weights, cross, preferred_element_type=jnp.float32)
        factor = jnp.where(slot < listed, scale, 0.0).astype(jnp.float32)
        result = jnp.transpose((lagged * factor).astype(jnp.bfloat16), (1, 0, 2))
        out = lax.dynamic_update_slice(out, result[None], (slot, 0, 0, 0))
    return out[None]


def solution(mesh):
    staged = mesh.shape["blk"] == 8
    placed = (P("blk", "freq", None, None, None), P("blk", None), P("blk"))
    return jax.shard_map(
        lambda s, po, pc: local(s, po, pc, staged),
        mesh=mesh,
        in_specs=placed,
        out_specs=P("blk", None, "freq", None, None),
        check_vma=False,
    )
```

```python
import math

import jax
import jax.numpy as jnp
import numpy as np
from jax import lax
from jax.sharding import PartitionSpec as P

F = 512
LAGS = 256
REACH = 4
SLOTS = 5
CHUNKS = 8
GROUP = 4


def from_behind(shard, axis, by):
    size = lax.axis_size(axis)
    return lax.ppermute(shard, axis, [(i, (i + by) % size) for i in range(size)])


def swap(shard, axis, mask):
    size = lax.axis_size(axis)
    return lax.ppermute(shard, axis, [(i, i ^ mask) for i in range(size)])


def lag_table(bins_order):
    shifted = jnp.arange(LAGS, dtype=jnp.int32) - LAGS // 2
    bins = jnp.asarray(bins_order, dtype=jnp.int32) + 1
    phase = jnp.mod(shifted[:, None] * bins[None, :], 2 * F).astype(jnp.float32) * (jnp.pi / F)
    return jnp.stack([jnp.cos(phase), -jnp.sin(phase)], axis=-1).astype(jnp.bfloat16)


def home_rows(own, start, width):
    freq_count, parts_count, windows, stations = own.shape
    flat = own.reshape(freq_count, parts_count * windows, stations)
    picked = lax.dynamic_slice_in_dim(jnp.transpose(flat, (0, 2, 1)), start, width, axis=1)
    turned = jnp.concatenate([-picked[..., windows:], picked[..., :windows]], axis=2)
    rows_t = jnp.concatenate([picked, turned], axis=1)
    group = GROUP if freq_count % GROUP == 0 else 1
    count, size_s, size_k = freq_count // group, rows_t.shape[1], rows_t.shape[2]
    blocks = rows_t.reshape(count, group, size_s, 1, size_k)
    eye = jnp.eye(group, dtype=rows_t.dtype).reshape(1, group, 1, group, 1)
    return (blocks * eye).reshape(count, group * size_s, group * size_k)


def cross_spectrum(rows_t, partner):
    freq_count, parts_count, windows, stations = partner.shape
    count = rows_t.shape[0]
    width = rows_t.shape[1] * count // freq_count // 2
    columns = partner.reshape(count, freq_count // count * parts_count * windows, stations)
    summed = jnp.einsum("fSk,fkt->fSt", rows_t, columns, preferred_element_type=jnp.float32)
    return (summed / windows).astype(jnp.bfloat16).reshape(freq_count, 2, width, stations)


def local(spectra, pair_offsets, pair_count, staged):
    own_part = spectra[0]
    local_freqs, _, _, stations = own_part.shape
    parts = lax.axis_size("freq")
    freq_total = local_freqs * parts
    chunks = CHUNKS if local_freqs % CHUNKS == 0 else 1
    piece = local_freqs // chunks
    width = stations // parts
    q = lax.axis_index("freq")
    b = lax.axis_index("blk")
    x_bit = (b // 2) % 2
    core = b % 2

    order = np.array(
        [qq * local_freqs + j * piece + i for j in range(chunks) for qq in range(parts) for i in range(piece)]
    )
    held = {"part/%d" % j: own_part[j * piece:(j + 1) * piece] for j in range(chunks)}
    crosses = {}
    depth = 4 if staged else 1
    for step in range(chunks + depth + 1):
        made = {}
        j = step
        if j < chunks:
            made["own/%d" % j] = lax.all_gather(held["part/%d" % j], "freq", axis=0, tiled=True)
        j = step - 1
        if 0 <= j < chunks:
            own = held["own/%d" % j]
            made["rows/%d" % j] = home_rows(own, q * width, width)
            if staged:
                made["r4/%d" % j] = swap(own, "blk", 4)
            else:
                for o in range(1, REACH + 1):
                    made["r%d/%d" % (o, j)] = from_behind(own, "blk", -o)
        if staged:
            j = step - 2
            if 0 <= j < chunks:
                made["r2/%d" % j] = swap(jnp.where(x_bit == 1, held["own/%d" % j], held["r4/%d" % j]), "blk", 2)
            j = step - 3
            if 0 <= j < chunks:
                made["r1/%d" % j] = swap(jnp.where(core == 1, held["own/%d" % j], held["r2/%d" % j]), "blk", 1)
                made["r3/%d" % j] = swap(jnp.where(core == 1, held["r2/%d" % j], held["r4/%d" % j]), "blk", 1)
        for key in list(held):
            if "/" not in key:
                continue
            name, j = key.split("/")[0], int(key.split("/")[-1])
            if name in ("own", "r1", "r2", "r3", "r4"):
                o = 0 if name == "own" else int(name[1])
                if "rows/%d" % j in held and (o, j) not in crosses:
                    part = cross_spectrum(held["rows/%d" % j], held[key])
                    name = "cross%d" % o
                    base = made.get(name, held.get(name))
                    if base is None:
                        base = jnp.zeros((freq_total, 2, width, stations), jnp.bfloat16)
                    made[name] = lax.dynamic_update_slice(base, part, (j * piece * parts, 0, 0, 0))
                    crosses[(o, j)] = True
        keep = dict(held)
        for j in range(chunks):
            if step >= j:
                keep.pop("part/%d" % j, None)
            if all((o, j) in crosses for o in range(REACH + 1)):
                for name in ("own", "rows", "r1", "r2", "r3", "r4"):
                    keep.pop("%s/%d" % (name, j), None)
        keep.update(made)
        held = lax.optimization_barrier(keep)

    offsets = pair_offsets[0]
    listed = pair_count[0]
    weights = lag_table(order).reshape(LAGS, freq_total * 2)
    scale = math.sqrt(2.0 / freq_total)
    out = jnp.zeros((SLOTS, width, LAGS, stations), jnp.bfloat16)
    for o in range(REACH + 1):
        slot = jnp.argmax(offsets == o).astype(jnp.int32)
        cross = held["cross%d" % o].reshape(freq_total * 2, width, stations)
        lagged = jnp.einsum("lK,Kst->lst", weights, cross, preferred_element_type=jnp.float32)
        factor = jnp.where(slot < listed, scale, 0.0).astype(jnp.float32)
        result = jnp.transpose((lagged * factor).astype(jnp.bfloat16), (1, 0, 2))
        out = lax.dynamic_update_slice(out, result[None], (slot, 0, 0, 0))
    return out[None]


def solution(mesh):
    staged = mesh.shape["blk"] == 8
    placed = (P("blk", "freq", None, None, None), P("blk", None), P("blk"))
    return jax.shard_map(
        lambda s, po, pc: local(s, po, pc, staged),
        mesh=mesh,
        in_specs=placed,
        out_specs=P("blk", None, "freq", None, None),
        check_vma=False,
    )
```

```python
import math

import jax
import jax.numpy as jnp
import numpy as np
from jax import lax
from jax.sharding import PartitionSpec as P

F = 512
LAGS = 256
REACH = 4
SLOTS = 5
CHUNKS = 8


def from_behind(shard, axis, by):
    size = lax.axis_size(axis)
    return lax.ppermute(shard, axis, [(i, (i + by) % size) for i in range(size)])


def swap(shard, axis, mask):
    size = lax.axis_size(axis)
    return lax.ppermute(shard, axis, [(i, i ^ mask) for i in range(size)])


def lag_table(bins_order):
    shifted = jnp.arange(LAGS, dtype=jnp.int32) - LAGS // 2
    bins = jnp.asarray(bins_order, dtype=jnp.int32) + 1
    phase = jnp.mod(shifted[:, None] * bins[None, :], 2 * F).astype(jnp.float32) * (jnp.pi / F)
    return jnp.stack([jnp.cos(phase), -jnp.sin(phase)], axis=-1).astype(jnp.bfloat16)


def home_rows(own, start, width):
    freq_count, parts_count, windows, stations = own.shape
    flat = own.reshape(freq_count, parts_count * windows, stations)
    picked = lax.dynamic_slice_in_dim(jnp.transpose(flat, (0, 2, 1)), start, width, axis=1)
    turned = jnp.concatenate([-picked[..., windows:], picked[..., :windows]], axis=2)
    return jnp.concatenate([picked, turned], axis=1)


def cross_spectrum(rows_t, partner):
    freq_count, parts_count, windows, stations = partner.shape
    width = rows_t.shape[1] // 2
    columns = partner.reshape(freq_count, parts_count * windows, stations)
    summed = jnp.einsum("fSk,fkt->fSt", rows_t, columns, preferred_element_type=jnp.float32)
    return (summed / windows).astype(jnp.bfloat16).reshape(freq_count, 2, width, stations)


def local(spectra, pair_offsets, pair_count, staged):
    own_part = spectra[0]
    local_freqs, _, _, stations = own_part.shape
    parts = lax.axis_size("freq")
    freq_total = local_freqs * parts
    chunks = CHUNKS if local_freqs % CHUNKS == 0 else 1
    piece = local_freqs // chunks
    width = stations // parts
    q = lax.axis_index("freq")
    b = lax.axis_index("blk")
    x_bit = (b // 2) % 2
    core = b % 2

    quarter = np.array([qq for j in range(chunks) for qq in range(parts) for i in range(piece)])
    within = np.array([j * piece + i for j in range(chunks) for qq in range(parts) for i in range(piece)])
    if staged:
        order = ((jnp.asarray(quarter, jnp.int32) + q) % parts) * local_freqs + jnp.asarray(within, jnp.int32)
    else:
        order = quarter * local_freqs + within
    held = {"part/%d" % j: own_part[j * piece:(j + 1) * piece] for j in range(chunks)}
    crosses = {}
    depth = 4 if staged else 1
    for step in range(chunks + depth + 1):
        made = {}
        j = step
        if j < chunks:
            piece_j = held["part/%d" % j]
            if staged:
                gathered = [piece_j] + [from_behind(piece_j, "freq", -d) for d in range(1, parts)]
                made["own/%d" % j] = jnp.concatenate(gathered, axis=0)
            else:
                made["own/%d" % j] = lax.all_gather(piece_j, "freq", axis=0, tiled=True)
        j = step - 1
        if 0 <= j < chunks:
            own = held["own/%d" % j]
            made["rows/%d" % j] = home_rows(own, q * width, width)
            if staged:
                made["r4/%d" % j] = swap(own, "blk", 4)
            else:
                for o in range(1, REACH + 1):
                    made["r%d/%d" % (o, j)] = from_behind(own, "blk", -o)
        if staged:
            j = step - 2
            if 0 <= j < chunks:
                made["r2/%d" % j] = swap(jnp.where(x_bit == 1, held["own/%d" % j], held["r4/%d" % j]), "blk", 2)
            j = step - 3
            if 0 <= j < chunks:
                made["r1/%d" % j] = swap(jnp.where(core == 1, held["own/%d" % j], held["r2/%d" % j]), "blk", 1)
                made["r3/%d" % j] = swap(jnp.where(core == 1, held["r2/%d" % j], held["r4/%d" % j]), "blk", 1)
        for key in list(held):
            if "/" not in key:
                continue
            name, j = key.split("/")[0], int(key.split("/")[-1])
            if name in ("own", "r1", "r2", "r3", "r4"):
                o = 0 if name == "own" else int(name[1])
                if "rows/%d" % j in held and (o, j) not in crosses:
                    part = cross_spectrum(held["rows/%d" % j], held[key])
                    name = "cross%d" % o
                    base = made.get(name, held.get(name))
                    if base is None:
                        base = jnp.zeros((freq_total, 2, width, stations), jnp.bfloat16)
                    made[name] = lax.dynamic_update_slice(base, part, (j * piece * parts, 0, 0, 0))
                    crosses[(o, j)] = True
        keep = dict(held)
        for j in range(chunks):
            if step >= j:
                keep.pop("part/%d" % j, None)
            if all((o, j) in crosses for o in range(REACH + 1)):
                for name in ("own", "rows", "r1", "r2", "r3", "r4"):
                    keep.pop("%s/%d" % (name, j), None)
        keep.update(made)
        held = lax.optimization_barrier(keep)

    offsets = pair_offsets[0]
    listed = pair_count[0]
    weights = lag_table(order).reshape(LAGS, freq_total * 2)
    scale = math.sqrt(2.0 / freq_total)
    out = jnp.zeros((SLOTS, width, LAGS, stations), jnp.bfloat16)
    for o in range(REACH + 1):
        slot = jnp.argmax(offsets == o).astype(jnp.int32)
        cross = held["cross%d" % o].reshape(freq_total * 2, width, stations)
        lagged = jnp.einsum("lK,Kst->lst", weights, cross, preferred_element_type=jnp.float32)
        factor = jnp.where(slot < listed, scale, 0.0).astype(jnp.float32)
        result = jnp.transpose((lagged * factor).astype(jnp.bfloat16), (1, 0, 2))
        out = lax.dynamic_update_slice(out, result[None], (slot, 0, 0, 0))
    return out[None]


def solution(mesh):
    staged = mesh.shape["blk"] == 8
    placed = (P("blk", "freq", None, None, None), P("blk", None), P("blk"))
    return jax.shard_map(
        lambda s, po, pc: local(s, po, pc, staged),
        mesh=mesh,
        in_specs=placed,
        out_specs=P("blk", None, "freq", None, None),
        check_vma=False,
    )
```

```python
import math

import jax
import jax.numpy as jnp
import numpy as np
from jax import lax
from jax.sharding import PartitionSpec as P

F = 512
LAGS = 256
REACH = 4
SLOTS = 5
CHUNKS = 8


def from_behind(shard, axis, by):
    size = lax.axis_size(axis)
    return lax.ppermute(shard, axis, [(i, (i + by) % size) for i in range(size)])


def swap(shard, axis, mask):
    size = lax.axis_size(axis)
    return lax.ppermute(shard, axis, [(i, i ^ mask) for i in range(size)])


def lag_table(bins_order):
    shifted = jnp.arange(LAGS, dtype=jnp.int32) - LAGS // 2
    bins = jnp.asarray(bins_order, dtype=jnp.int32) + 1
    phase = jnp.mod(shifted[:, None] * bins[None, :], 2 * F).astype(jnp.float32) * (jnp.pi / F)
    return jnp.stack([jnp.cos(phase), -jnp.sin(phase)], axis=-1).astype(jnp.bfloat16)


def home_rows(own, start, width):
    freq_count, parts_count, windows, stations = own.shape
    flat = own.reshape(freq_count, parts_count * windows, stations)
    picked = lax.dynamic_slice_in_dim(jnp.transpose(flat, (0, 2, 1)), start, width, axis=1)
    turned = jnp.concatenate([-picked[..., windows:], picked[..., :windows]], axis=2)
    return jnp.concatenate([picked, turned], axis=1)


def cross_spectrum(rows_t, partner):
    freq_count, parts_count, windows, stations = partner.shape
    width = rows_t.shape[1] // 2
    columns = partner.reshape(freq_count, parts_count * windows, stations)
    summed = jnp.einsum("fSk,fkt->fSt", rows_t, columns, preferred_element_type=jnp.float32)
    return (summed / windows).astype(jnp.bfloat16).reshape(freq_count, 2, width, stations)


def local(spectra, pair_offsets, pair_count, staged):
    own_part = spectra[0]
    local_freqs, _, _, stations = own_part.shape
    parts = lax.axis_size("freq")
    freq_total = local_freqs * parts
    chunks = CHUNKS if local_freqs % CHUNKS == 0 else 1
    piece = local_freqs // chunks
    width = stations // parts
    q = lax.axis_index("freq")
    b = lax.axis_index("blk")
    x_bit = (b // 2) % 2
    core = b % 2

    order = np.array(
        [qq * local_freqs + j * piece + i for j in range(chunks) for qq in range(parts) for i in range(piece)]
    )
    held = {"part/%d" % j: own_part[j * piece:(j + 1) * piece] for j in range(chunks)}
    crosses = {}
    depth = 4 if staged else 1
    for step in range(chunks + depth + 1):
        made = {}
        j = step
        if j < chunks:
            made["own/%d" % j] = lax.all_gather(held["part/%d" % j], "freq", axis=0, tiled=True)
        j = step - 1
        if 0 <= j < chunks:
            own = held["own/%d" % j]
            made["rows/%d" % j] = home_rows(own, q * width, width)
            if staged:
                made["r4/%d" % j] = swap(own, "blk", 4)
            else:
                for o in range(1, REACH + 1):
                    made["r%d/%d" % (o, j)] = from_behind(own, "blk", -o)
        if staged:
            j = step - 2
            if 0 <= j < chunks:
                made["r2/%d" % j] = swap(jnp.where(x_bit == 1, held["own/%d" % j], held["r4/%d" % j]), "blk", 2)
            j = step - 3
            if 0 <= j < chunks:
                made["r1/%d" % j] = swap(jnp.where(core == 1, held["own/%d" % j], held["r2/%d" % j]), "blk", 1)
                made["r3/%d" % j] = swap(jnp.where(core == 1, held["r2/%d" % j], held["r4/%d" % j]), "blk", 1)
        for key in list(held):
            if "/" not in key:
                continue
            name, j = key.split("/")[0], int(key.split("/")[-1])
            if name in ("own", "r1", "r2", "r3", "r4"):
                o = 0 if name == "own" else int(name[1])
                if "rows/%d" % j in held and (o, j) not in crosses:
                    part = cross_spectrum(held["rows/%d" % j], held[key])
                    name = "cross%d" % o
                    base = made.get(name, held.get(name))
                    if base is None:
                        base = jnp.zeros((freq_total, 2, width, stations), jnp.bfloat16)
                    made[name] = lax.dynamic_update_slice(base, part, (j * piece * parts, 0, 0, 0))
                    crosses[(o, j)] = True
        keep = dict(held)
        for j in range(chunks):
            if step >= j:
                keep.pop("part/%d" % j, None)
            if all((o, j) in crosses for o in range(REACH + 1)):
                for name in ("own", "rows", "r1", "r2", "r3", "r4"):
                    keep.pop("%s/%d" % (name, j), None)
            elif "r1/%d" % j in made or "r1/%d" % j in held:
                for name, o in (("own", 0), ("r2", 2), ("r4", 4)):
                    if (o, j) in crosses and "r3/%d" % j in keep or (o, j) in crosses and "r3/%d" % j in made:
                        keep.pop("%s/%d" % (name, j), None)
        keep.update(made)
        held = lax.optimization_barrier(keep)

    offsets = pair_offsets[0]
    listed = pair_count[0]
    weights = lag_table(order).reshape(LAGS, freq_total * 2)
    scale = math.sqrt(2.0 / freq_total)
    out = jnp.zeros((SLOTS, width, LAGS, stations), jnp.bfloat16)
    for o in range(REACH + 1):
        slot = jnp.argmax(offsets == o).astype(jnp.int32)
        cross = held["cross%d" % o].reshape(freq_total * 2, width, stations)
        lagged = jnp.einsum("lK,Kst->lst", weights, cross, preferred_element_type=jnp.float32)
        factor = jnp.where(slot < listed, scale, 0.0).astype(jnp.float32)
        result = jnp.transpose((lagged * factor).astype(jnp.bfloat16), (1, 0, 2))
        out = lax.dynamic_update_slice(out, result[None], (slot, 0, 0, 0))
    return out[None]


def solution(mesh):
    staged = mesh.shape["blk"] == 8
    placed = (P("blk", "freq", None, None, None), P("blk", None), P("blk"))
    return jax.shard_map(
        lambda s, po, pc: local(s, po, pc, staged),
        mesh=mesh,
        in_specs=placed,
        out_specs=P("blk", None, "freq", None, None),
        check_vma=False,
    )
```

```python
import math

import jax
import jax.numpy as jnp
import numpy as np
from jax import lax
from jax.sharding import PartitionSpec as P

F = 512
LAGS = 256
REACH = 4
SLOTS = 5
CHUNKS = 8


def from_behind(shard, axis, by):
    size = lax.axis_size(axis)
    return lax.ppermute(shard, axis, [(i, (i + by) % size) for i in range(size)])


def swap(shard, axis, mask):
    size = lax.axis_size(axis)
    return lax.ppermute(shard, axis, [(i, i ^ mask) for i in range(size)])


def lag_table(bins_order):
    shifted = jnp.arange(LAGS, dtype=jnp.int32) - LAGS // 2
    bins = jnp.asarray(bins_order, dtype=jnp.int32) + 1
    phase = jnp.mod(shifted[:, None] * bins[None, :], 2 * F).astype(jnp.float32) * (jnp.pi / F)
    return jnp.stack([jnp.cos(phase), -jnp.sin(phase)], axis=-1).astype(jnp.bfloat16)


def home_rows(own, start, width):
    freq_count, parts_count, windows, stations = own.shape
    flat = own.reshape(freq_count, parts_count * windows, stations)
    picked = lax.dynamic_slice_in_dim(jnp.transpose(flat, (0, 2, 1)), start, width, axis=1)
    turned = jnp.concatenate([-picked[..., windows:], picked[..., :windows]], axis=2)
    return jnp.concatenate([picked, turned], axis=1)


def cross_spectrum(rows_t, partner):
    freq_count, parts_count, windows, stations = partner.shape
    width = rows_t.shape[1] // 2
    columns = partner.reshape(freq_count, parts_count * windows, stations)
    summed = jnp.einsum("fSk,fkt->fSt", rows_t, columns, preferred_element_type=jnp.float32)
    return (summed / windows).astype(jnp.bfloat16).reshape(freq_count, 2, width, stations)


def local(spectra, pair_offsets, pair_count, staged):
    own_part = spectra[0]
    local_freqs, _, _, stations = own_part.shape
    parts = lax.axis_size("freq")
    freq_total = local_freqs * parts
    chunks = CHUNKS if local_freqs % CHUNKS == 0 else 1
    piece = local_freqs // chunks
    width = stations // parts
    q = lax.axis_index("freq")
    b = lax.axis_index("blk")
    x_bit = (b // 2) % 2
    core = b % 2

    coarse = 2 if staged and chunks % 2 == 0 else 1
    gathered_piece = piece * coarse
    rows_per_chunk = piece * parts
    order = []
    for j in range(chunks):
        big, h = j // coarse, j % coarse
        for n in range(h * rows_per_chunk, (h + 1) * rows_per_chunk):
            order.append((n // gathered_piece) * local_freqs + big * gathered_piece + n % gathered_piece)
    order = np.array(order)
    held = {"part/%d" % j: own_part[j * gathered_piece:(j + 1) * gathered_piece] for j in range(chunks // coarse)}
    shift = coarse
    pending = {}
    crosses = {}
    depth = 4 if staged else 1
    for step in range(chunks + depth + shift):
        made = dict(pending)
        pending = {}
        if step % coarse == 0 and step // coarse < chunks // coarse:
            big = step // coarse
            whole = lax.all_gather(held["part/%d" % big], "freq", axis=0, tiled=True)
            for h in range(coarse):
                piece_rows = whole[h * rows_per_chunk:(h + 1) * rows_per_chunk]
                target = pending if coarse > 1 else made
                target["own/%d" % (big * coarse + h)] = piece_rows
        j = step - shift
        if 0 <= j < chunks:
            own = held["own/%d" % j]
            made["rows/%d" % j] = home_rows(own, q * width, width)
            if staged:
                made["r4/%d" % j] = swap(own, "blk", 4)
            else:
                for o in range(1, REACH + 1):
                    made["r%d/%d" % (o, j)] = from_behind(own, "blk", -o)
        if staged:
            j = step - shift - 1
            if 0 <= j < chunks:
                made["r2/%d" % j] = swap(jnp.where(x_bit == 1, held["own/%d" % j], held["r4/%d" % j]), "blk", 2)
            j = step - shift - 2
            if 0 <= j < chunks:
                made["r1/%d" % j] = swap(jnp.where(core == 1, held["own/%d" % j], held["r2/%d" % j]), "blk", 1)
                made["r3/%d" % j] = swap(jnp.where(core == 1, held["r2/%d" % j], held["r4/%d" % j]), "blk", 1)
        for key in list(held):
            if "/" not in key:
                continue
            name, j = key.split("/")[0], int(key.split("/")[-1])
            if name in ("own", "r1", "r2", "r3", "r4"):
                o = 0 if name == "own" else int(name[1])
                if "rows/%d" % j in held and (o, j) not in crosses:
                    part = cross_spectrum(held["rows/%d" % j], held[key])
                    name = "cross%d" % o
                    base = made.get(name, held.get(name))
                    if base is None:
                        base = jnp.zeros((freq_total, 2, width, stations), jnp.bfloat16)
                    made[name] = lax.dynamic_update_slice(base, part, (j * piece * parts, 0, 0, 0))
                    crosses[(o, j)] = True
        keep = dict(held)
        for j in range(chunks):
            if step >= j * coarse:
                keep.pop("part/%d" % j, None)
            if all((o, j) in crosses for o in range(REACH + 1)):
                for name in ("own", "rows", "r1", "r2", "r3", "r4"):
                    keep.pop("%s/%d" % (name, j), None)
        keep.update(made)
        held = lax.optimization_barrier(keep)

    offsets = pair_offsets[0]
    listed = pair_count[0]
    weights = lag_table(order).reshape(LAGS, freq_total * 2)
    scale = math.sqrt(2.0 / freq_total)
    out = jnp.zeros((SLOTS, width, LAGS, stations), jnp.bfloat16)
    for o in range(REACH + 1):
        slot = jnp.argmax(offsets == o).astype(jnp.int32)
        cross = held["cross%d" % o].reshape(freq_total * 2, width, stations)
        lagged = jnp.einsum("lK,Kst->lst", weights, cross, preferred_element_type=jnp.float32)
        factor = jnp.where(slot < listed, scale, 0.0).astype(jnp.float32)
        result = jnp.transpose((lagged * factor).astype(jnp.bfloat16), (1, 0, 2))
        out = lax.dynamic_update_slice(out, result[None], (slot, 0, 0, 0))
    return out[None]


def solution(mesh):
    staged = mesh.shape["blk"] == 8
    placed = (P("blk", "freq", None, None, None), P("blk", None), P("blk"))
    return jax.shard_map(
        lambda s, po, pc: local(s, po, pc, staged),
        mesh=mesh,
        in_specs=placed,
        out_specs=P("blk", None, "freq", None, None),
        check_vma=False,
    )
```

```python
import math

import jax
import jax.numpy as jnp
import numpy as np
from jax import lax
from jax.sharding import PartitionSpec as P

F = 512
LAGS = 256
REACH = 4
SLOTS = 5
CHUNKS = 8


def from_behind(shard, axis, by):
    size = lax.axis_size(axis)
    return lax.ppermute(shard, axis, [(i, (i + by) % size) for i in range(size)])


def swap(shard, axis, mask):
    size = lax.axis_size(axis)
    return lax.ppermute(shard, axis, [(i, i ^ mask) for i in range(size)])


def pick(flag, when_set, otherwise):
    return lax.cond(flag, lambda a, b: a, lambda a, b: b, when_set, otherwise)


def lag_table(bins_order):
    shifted = jnp.arange(LAGS, dtype=jnp.int32) - LAGS // 2
    bins = jnp.asarray(bins_order, dtype=jnp.int32) + 1
    phase = jnp.mod(shifted[:, None] * bins[None, :], 2 * F).astype(jnp.float32) * (jnp.pi / F)
    return jnp.stack([jnp.cos(phase), -jnp.sin(phase)], axis=-1).astype(jnp.bfloat16)


def home_rows(own, start, width):
    freq_count, parts_count, windows, stations = own.shape
    flat = own.reshape(freq_count, parts_count * windows, stations)
    picked = lax.dynamic_slice_in_dim(jnp.transpose(flat, (0, 2, 1)), start, width, axis=1)
    turned = jnp.concatenate([-picked[..., windows:], picked[..., :windows]], axis=2)
    return jnp.concatenate([picked, turned], axis=1)


def cross_spectrum(rows_t, partner):
    freq_count, parts_count, windows, stations = partner.shape
    width = rows_t.shape[1] // 2
    columns = partner.reshape(freq_count, parts_count * windows, stations)
    summed = jnp.einsum("fSk,fkt->fSt", rows_t, columns, preferred_element_type=jnp.float32)
    return (summed / windows).astype(jnp.bfloat16).reshape(freq_count, 2, width, stations)


def local(spectra, pair_offsets, pair_count, staged):
    own_part = spectra[0]
    local_freqs, _, _, stations = own_part.shape
    parts = lax.axis_size("freq")
    freq_total = local_freqs * parts
    chunks = CHUNKS if local_freqs % CHUNKS == 0 else 1
    piece = local_freqs // chunks
    width = stations // parts
    q = lax.axis_index("freq")
    b = lax.axis_index("blk")
    x_bit = (b // 2) % 2
    core = b % 2

    order = np.array(
        [qq * local_freqs + j * piece + i for j in range(chunks) for qq in range(parts) for i in range(piece)]
    )
    held = {"part/%d" % j: own_part[j * piece:(j + 1) * piece] for j in range(chunks)}
    crosses = {}
    depth = 4 if staged else 1
    for step in range(chunks + depth + 1):
        made = {}
        j = step
        if j < chunks:
            made["own/%d" % j] = lax.all_gather(held["part/%d" % j], "freq", axis=0, tiled=True)
        j = step - 1
        if 0 <= j < chunks:
            own = held["own/%d" % j]
            made["rows/%d" % j] = home_rows(own, q * width, width)
            if staged:
                made["r4/%d" % j] = swap(own, "blk", 4)
            else:
                for o in range(1, REACH + 1):
                    made["r%d/%d" % (o, j)] = from_behind(own, "blk", -o)
        if staged:
            j = step - 2
            if 0 <= j < chunks:
                made["r2/%d" % j] = swap(pick(x_bit == 1, held["own/%d" % j], held["r4/%d" % j]), "blk", 2)
            j = step - 3
            if 0 <= j < chunks:
                made["r1/%d" % j] = swap(pick(core == 1, held["own/%d" % j], held["r2/%d" % j]), "blk", 1)
                made["r3/%d" % j] = swap(pick(core == 1, held["r2/%d" % j], held["r4/%d" % j]), "blk", 1)
        for key in list(held):
            if "/" not in key:
                continue
            name, j = key.split("/")[0], int(key.split("/")[-1])
            if name in ("own", "r1", "r2", "r3", "r4"):
                o = 0 if name == "own" else int(name[1])
                if "rows/%d" % j in held and (o, j) not in crosses:
                    part = cross_spectrum(held["rows/%d" % j], held[key])
                    name = "cross%d" % o
                    base = made.get(name, held.get(name))
                    if base is None:
                        base = jnp.zeros((freq_total, 2, width, stations), jnp.bfloat16)
                    made[name] = lax.dynamic_update_slice(base, part, (j * piece * parts, 0, 0, 0))
                    crosses[(o, j)] = True
        keep = dict(held)
        for j in range(chunks):
            if step >= j:
                keep.pop("part/%d" % j, None)
            if all((o, j) in crosses for o in range(REACH + 1)):
                for name in ("own", "rows", "r1", "r2", "r3", "r4"):
                    keep.pop("%s/%d" % (name, j), None)
        keep.update(made)
        held = lax.optimization_barrier(keep)

    offsets = pair_offsets[0]
    listed = pair_count[0]
    weights = lag_table(order).reshape(LAGS, freq_total * 2)
    scale = math.sqrt(2.0 / freq_total)
    out = jnp.zeros((SLOTS, width, LAGS, stations), jnp.bfloat16)
    for o in range(REACH + 1):
        slot = jnp.argmax(offsets == o).astype(jnp.int32)
        cross = held["cross%d" % o].reshape(freq_total * 2, width, stations)
        lagged = jnp.einsum("lK,Kst->lst", weights, cross, preferred_element_type=jnp.float32)
        factor = jnp.where(slot < listed, scale, 0.0).astype(jnp.float32)
        result = jnp.transpose((lagged * factor).astype(jnp.bfloat16), (1, 0, 2))
        out = lax.dynamic_update_slice(out, result[None], (slot, 0, 0, 0))
    return out[None]


def solution(mesh):
    staged = mesh.shape["blk"] == 8
    placed = (P("blk", "freq", None, None, None), P("blk", None), P("blk"))
    return jax.shard_map(
        lambda s, po, pc: local(s, po, pc, staged),
        mesh=mesh,
        in_specs=placed,
        out_specs=P("blk", None, "freq", None, None),
        check_vma=False,
    )
```

```python
import math

import jax
import jax.numpy as jnp
import numpy as np
from jax import lax
from jax.sharding import PartitionSpec as P

F = 512
LAGS = 256
REACH = 4
SLOTS = 5
CHUNKS = 8


def from_behind(shard, axis, by):
    size = lax.axis_size(axis)
    return lax.ppermute(shard, axis, [(i, (i + by) % size) for i in range(size)])


def swap(shard, axis, mask):
    size = lax.axis_size(axis)
    return lax.ppermute(shard, axis, [(i, i ^ mask) for i in range(size)])


def lag_table(bins_order):
    shifted = jnp.arange(LAGS, dtype=jnp.int32) - LAGS // 2
    bins = jnp.asarray(bins_order, dtype=jnp.int32) + 1
    phase = jnp.mod(shifted[:, None] * bins[None, :], 2 * F).astype(jnp.float32) * (jnp.pi / F)
    return jnp.stack([jnp.cos(phase), -jnp.sin(phase)], axis=-1).astype(jnp.bfloat16)


def home_rows(own, start, width):
    freq_count, parts_count, windows, stations = own.shape
    flat = own.reshape(freq_count, parts_count * windows, stations)
    picked = lax.dynamic_slice_in_dim(jnp.transpose(flat, (0, 2, 1)), start, width, axis=1)
    turned = jnp.concatenate([-picked[..., windows:], picked[..., :windows]], axis=2)
    return jnp.concatenate([picked, turned], axis=1)


def cross_spectrum(rows_t, partner):
    freq_count, parts_count, windows, stations = partner.shape
    width = rows_t.shape[1] // 2
    columns = partner.reshape(freq_count, parts_count * windows, stations)
    summed = jnp.einsum("fSk,fkt->fSt", rows_t, columns, preferred_element_type=jnp.float32)
    return (summed / windows).astype(jnp.bfloat16).reshape(freq_count, 2, width, stations)


def local(spectra, pair_offsets, pair_count, staged):
    own_part = spectra[0]
    local_freqs, _, _, stations = own_part.shape
    parts = lax.axis_size("freq")
    freq_total = local_freqs * parts
    chunks = CHUNKS if local_freqs % CHUNKS == 0 else 1
    piece = local_freqs // chunks
    width = stations // parts
    q = lax.axis_index("freq")
    b = lax.axis_index("blk")
    x_bit = (b // 2) % 2
    core = b % 2

    order = np.array(
        [qq * local_freqs + j * piece + i for j in range(chunks) for qq in range(parts) for i in range(piece)]
    )
    held = {}
    crosses = {}
    depth = 4 if staged else 1
    for step in range(chunks + depth + 1):
        made = {}
        j = step
        if j < chunks:
            made["own/%d" % j] = lax.all_gather(own_part[j * piece:(j + 1) * piece], "freq", axis=0, tiled=True)
        j = step - 1
        if 0 <= j < chunks:
            own = held["own/%d" % j]
            made["rows/%d" % j] = home_rows(own, q * width, width)
            if staged:
                made["r4/%d" % j] = swap(own, "blk", 4)
            else:
                for o in range(1, REACH + 1):
                    made["r%d/%d" % (o, j)] = from_behind(own, "blk", -o)
        if staged:
            j = step - 2
            if 0 <= j < chunks:
                made["r2/%d" % j] = swap(jnp.where(x_bit == 1, held["own/%d" % j], held["r4/%d" % j]), "blk", 2)
            j = step - 3
            if 0 <= j < chunks:
                made["r1/%d" % j] = swap(jnp.where(core == 1, held["own/%d" % j], held["r2/%d" % j]), "blk", 1)
                made["r3/%d" % j] = swap(jnp.where(core == 1, held["r2/%d" % j], held["r4/%d" % j]), "blk", 1)
        for key in list(held):
            if "/" not in key:
                continue
            name, j = key.split("/")[0], int(key.split("/")[-1])
            if name in ("own", "r1", "r2", "r3", "r4"):
                o = 0 if name == "own" else int(name[1])
                if "rows/%d" % j in held and (o, j) not in crosses:
                    part = cross_spectrum(held["rows/%d" % j], held[key])
                    name = "cross%d" % o
                    base = made.get(name, held.get(name))
                    if base is None:
                        base = jnp.zeros((freq_total, 2, width, stations), jnp.bfloat16)
                    made[name] = lax.dynamic_update_slice(base, part, (j * piece * parts, 0, 0, 0))
                    crosses[(o, j)] = True
        keep = dict(held)
        for j in range(chunks):
            if step >= j:
                keep.pop("part/%d" % j, None)
            if all((o, j) in crosses for o in range(REACH + 1)):
                for name in ("own", "rows", "r1", "r2", "r3", "r4"):
                    keep.pop("%s/%d" % (name, j), None)
        keep.update(made)
        held = lax.optimization_barrier(keep)

    offsets = pair_offsets[0]
    listed = pair_count[0]
    weights = lag_table(order).reshape(LAGS, freq_total * 2)
    scale = math.sqrt(2.0 / freq_total)
    out = jnp.zeros((SLOTS, width, LAGS, stations), jnp.bfloat16)
    for o in range(REACH + 1):
        slot = jnp.argmax(offsets == o).astype(jnp.int32)
        cross = held["cross%d" % o].reshape(freq_total * 2, width, stations)
        lagged = jnp.einsum("lK,Kst->lst", weights, cross, preferred_element_type=jnp.float32)
        factor = jnp.where(slot < listed, scale, 0.0).astype(jnp.float32)
        result = jnp.transpose((lagged * factor).astype(jnp.bfloat16), (1, 0, 2))
        out = lax.dynamic_update_slice(out, result[None], (slot, 0, 0, 0))
    return out[None]


def solution(mesh):
    staged = mesh.shape["blk"] == 8
    placed = (P("blk", "freq", None, None, None), P("blk", None), P("blk"))
    return jax.shard_map(
        lambda s, po, pc: local(s, po, pc, staged),
        mesh=mesh,
        in_specs=placed,
        out_specs=P("blk", None, "freq", None, None),
        check_vma=False,
    )
```

```python
import math

import jax
import jax.numpy as jnp
import numpy as np
from jax import lax
from jax.sharding import PartitionSpec as P

F = 512
LAGS = 256
REACH = 4
SLOTS = 5
CHUNKS = 8


def from_behind(shard, axis, by):
    size = lax.axis_size(axis)
    return lax.ppermute(shard, axis, [(i, (i + by) % size) for i in range(size)])


def swap(shard, axis, mask):
    size = lax.axis_size(axis)
    return lax.ppermute(shard, axis, [(i, i ^ mask) for i in range(size)])


def lag_table(bins_order):
    shifted = jnp.arange(LAGS, dtype=jnp.int32) - LAGS // 2
    bins = jnp.asarray(bins_order, dtype=jnp.int32) + 1
    phase = jnp.mod(shifted[:, None] * bins[None, :], 2 * F).astype(jnp.float32) * (jnp.pi / F)
    return jnp.stack([jnp.cos(phase), -jnp.sin(phase)], axis=-1).astype(jnp.bfloat16)


def home_rows(own, start, width):
    freq_count, parts_count, windows, stations = own.shape
    flat = own.reshape(freq_count, parts_count * windows, stations)
    picked = lax.dynamic_slice_in_dim(jnp.transpose(flat, (0, 2, 1)), start, width, axis=1)
    turned = jnp.concatenate([-picked[..., windows:], picked[..., :windows]], axis=2)
    return jnp.concatenate([picked, turned], axis=1)


def cross_spectrum(rows_t, partner):
    freq_count, parts_count, windows, stations = partner.shape
    width = rows_t.shape[1] // 2
    columns = partner.reshape(freq_count, parts_count * windows, stations)
    summed = jnp.einsum("fSk,fkt->fSt", rows_t, columns, preferred_element_type=jnp.float32)
    return (summed / windows).astype(jnp.bfloat16).reshape(freq_count, 2, width, stations)


def local(spectra, pair_offsets, pair_count, staged):
    own_part = spectra[0]
    local_freqs, _, _, stations = own_part.shape
    parts = lax.axis_size("freq")
    freq_total = local_freqs * parts
    chunks = CHUNKS if local_freqs % CHUNKS == 0 else 1
    piece = local_freqs // chunks
    width = stations // parts
    q = lax.axis_index("freq")
    b = lax.axis_index("blk")
    x_bit = (b // 2) % 2
    core = b % 2

    order = np.array(
        [qq * local_freqs + j * piece + i for j in range(chunks) for qq in range(parts) for i in range(piece)]
    )
    held = {"part/%d" % j: own_part[j * piece:(j + 1) * piece] for j in range(chunks)}
    crosses = {}
    depth = 4 if staged else 1
    for step in range(chunks + depth + 1):
        made = {}
        j = step
        if j < chunks:
            made["own/%d" % j] = lax.all_gather(held["part/%d" % j], "freq", axis=0, tiled=True)
        j = step - 1
        if 0 <= j < chunks:
            own = held["own/%d" % j]
            made["rows/%d" % j] = home_rows(own, q * width, width)
            if staged:
                made["r4/%d" % j] = swap(own, "blk", 4)
            else:
                for o in range(1, REACH + 1):
                    made["r%d/%d" % (o, j)] = from_behind(own, "blk", -o)
        if staged:
            j = step - 2
            if 0 <= j < chunks:
                made["r2/%d" % j] = swap(jnp.where(x_bit == 1, held["own/%d" % j], held["r4/%d" % j]), "blk", 2)
            j = step - 3
            if 0 <= j < chunks:
                made["r1/%d" % j] = swap(jnp.where(core == 1, held["own/%d" % j], held["r2/%d" % j]), "blk", 1)
                made["r3/%d" % j] = swap(jnp.where(core == 1, held["r2/%d" % j], held["r4/%d" % j]), "blk", 1)
        for key in list(held):
            if "/" not in key:
                continue
            name, j = key.split("/")[0], int(key.split("/")[-1])
            if name in ("own", "r1", "r2", "r3", "r4"):
                o = 0 if name == "own" else int(name[1])
                if "rows/%d" % j in held and (o, j) not in crosses:
                    part = cross_spectrum(held["rows/%d" % j], held[key])
                    name = "cross%d" % o
                    base = made.get(name, held.get(name))
                    start = j * piece * parts
                    if base is None:
                        spread = ((start, freq_total - start - part.shape[0]), (0, 0), (0, 0), (0, 0))
                        made[name] = jnp.pad(part, spread)
                    else:
                        made[name] = lax.dynamic_update_slice(base, part, (start, 0, 0, 0))
                    crosses[(o, j)] = True
        keep = dict(held)
        for j in range(chunks):
            if step >= j:
                keep.pop("part/%d" % j, None)
            if all((o, j) in crosses for o in range(REACH + 1)):
                for name in ("own", "rows", "r1", "r2", "r3", "r4"):
                    keep.pop("%s/%d" % (name, j), None)
        keep.update(made)
        held = lax.optimization_barrier(keep)

    offsets = pair_offsets[0]
    listed = pair_count[0]
    weights = lag_table(order).reshape(LAGS, freq_total * 2)
    scale = math.sqrt(2.0 / freq_total)
    out = jnp.zeros((SLOTS, width, LAGS, stations), jnp.bfloat16)
    for o in range(REACH + 1):
        slot = jnp.argmax(offsets == o).astype(jnp.int32)
        cross = held["cross%d" % o].reshape(freq_total * 2, width, stations)
        lagged = jnp.einsum("lK,Kst->lst", weights, cross, preferred_element_type=jnp.float32)
        factor = jnp.where(slot < listed, scale, 0.0).astype(jnp.float32)
        result = jnp.transpose((lagged * factor).astype(jnp.bfloat16), (1, 0, 2))
        out = lax.dynamic_update_slice(out, result[None], (slot, 0, 0, 0))
    return out[None]


def solution(mesh):
    staged = mesh.shape["blk"] == 8
    placed = (P("blk", "freq", None, None, None), P("blk", None), P("blk"))
    return jax.shard_map(
        lambda s, po, pc: local(s, po, pc, staged),
        mesh=mesh,
        in_specs=placed,
        out_specs=P("blk", None, "freq", None, None),
        check_vma=False,
    )
```

```python
import math

import jax
import jax.numpy as jnp
import numpy as np
from jax import lax
from jax.sharding import PartitionSpec as P

F = 512
LAGS = 256
REACH = 4
SLOTS = 5
CHUNKS = 8


def from_behind(shard, axis, by):
    size = lax.axis_size(axis)
    return lax.ppermute(shard, axis, [(i, (i + by) % size) for i in range(size)])


def swap(shard, axis, mask):
    size = lax.axis_size(axis)
    return lax.ppermute(shard, axis, [(i, i ^ mask) for i in range(size)])


def lag_table(bins_order):
    shifted = jnp.arange(LAGS, dtype=jnp.int32) - LAGS // 2
    bins = jnp.asarray(bins_order, dtype=jnp.int32) + 1
    phase = jnp.mod(shifted[:, None] * bins[None, :], 2 * F).astype(jnp.float32) * (jnp.pi / F)
    return jnp.stack([jnp.cos(phase), -jnp.sin(phase)], axis=-1).astype(jnp.bfloat16)


def home_rows(own, start, width):
    freq_count, parts_count, windows, stations = own.shape
    flat = own.reshape(freq_count, parts_count * windows, stations)
    picked = lax.dynamic_slice_in_dim(jnp.transpose(flat, (0, 2, 1)), start, width, axis=1)
    turned = jnp.concatenate([-picked[..., windows:], picked[..., :windows]], axis=2)
    return jnp.concatenate([picked, turned], axis=1)


def cross_spectrum(rows_t, partner):
    freq_count, parts_count, windows, stations = partner.shape
    width = rows_t.shape[1] // 2
    columns = partner.reshape(freq_count, parts_count * windows, stations)
    summed = jnp.einsum("fSk,fkt->fSt", rows_t, columns, preferred_element_type=jnp.float32)
    return (summed / windows).astype(jnp.bfloat16).reshape(freq_count, 2, width, stations)


def local(spectra, pair_offsets, pair_count, staged):
    own_part = spectra[0]
    local_freqs, _, _, stations = own_part.shape
    parts = lax.axis_size("freq")
    freq_total = local_freqs * parts
    chunks = CHUNKS if local_freqs % CHUNKS == 0 else 1
    piece = local_freqs // chunks
    width = stations // parts
    q = lax.axis_index("freq")
    b = lax.axis_index("blk")
    x_bit = (b // 2) % 2
    core = b % 2

    order = np.array(
        [qq * local_freqs + j * piece + i for j in range(chunks) for qq in range(parts) for i in range(piece)]
    )
    held = {"part/%d" % j: own_part[j * piece:(j + 1) * piece] for j in range(chunks)}
    crosses = {}
    depth = 4 if staged else 1
    offsets = pair_offsets[0]
    listed = pair_count[0]
    weights = lag_table(order).reshape(LAGS, freq_total * 2)
    scale = math.sqrt(2.0 / freq_total)
    lag_done = set()

    def lag_into(out, o, buffer):
        slot = jnp.argmax(offsets == o).astype(jnp.int32)
        cross = buffer.reshape(freq_total * 2, width, stations)
        lagged = jnp.einsum("lK,Kst->lst", weights, cross, preferred_element_type=jnp.float32)
        factor = jnp.where(slot < listed, scale, 0.0).astype(jnp.float32)
        result = jnp.transpose((lagged * factor).astype(jnp.bfloat16), (1, 0, 2))
        return lax.dynamic_update_slice(out, result[None], (slot, 0, 0, 0))

    for step in range(chunks + depth + 1):
        made = {}
        for o in range(REACH + 1):
            if o not in lag_done and all((o, j) in crosses for j in range(chunks)):
                out = made.get("out", held.get("out"))
                if out is None:
                    out = jnp.zeros((SLOTS, width, LAGS, stations), jnp.bfloat16)
                made["out"] = lag_into(out, o, held["cross%d" % o])
                lag_done.add(o)
        j = step
        if j < chunks:
            made["own/%d" % j] = lax.all_gather(held["part/%d" % j], "freq", axis=0, tiled=True)
        j = step - 1
        if 0 <= j < chunks:
            own = held["own/%d" % j]
            made["rows/%d" % j] = home_rows(own, q * width, width)
            if staged:
                made["r4/%d" % j] = swap(own, "blk", 4)
            else:
                for o in range(1, REACH + 1):
                    made["r%d/%d" % (o, j)] = from_behind(own, "blk", -o)
        if staged:
            j = step - 2
            if 0 <= j < chunks:
                made["r2/%d" % j] = swap(jnp.where(x_bit == 1, held["own/%d" % j], held["r4/%d" % j]), "blk", 2)
            j = step - 3
            if 0 <= j < chunks:
                made["r1/%d" % j] = swap(jnp.where(core == 1, held["own/%d" % j], held["r2/%d" % j]), "blk", 1)
                made["r3/%d" % j] = swap(jnp.where(core == 1, held["r2/%d" % j], held["r4/%d" % j]), "blk", 1)
        for key in list(held):
            if "/" not in key:
                continue
            name, j = key.split("/")[0], int(key.split("/")[-1])
            if name in ("own", "r1", "r2", "r3", "r4"):
                o = 0 if name == "own" else int(name[1])
                if "rows/%d" % j in held and (o, j) not in crosses:
                    part = cross_spectrum(held["rows/%d" % j], held[key])
                    name = "cross%d" % o
                    base = made.get(name, held.get(name))
                    if base is None:
                        base = jnp.zeros((freq_total, 2, width, stations), jnp.bfloat16)
                    made[name] = lax.dynamic_update_slice(base, part, (j * piece * parts, 0, 0, 0))
                    crosses[(o, j)] = True
        keep = dict(held)
        for o in lag_done:
            keep.pop("cross%d" % o, None)
        for j in range(chunks):
            if step >= j:
                keep.pop("part/%d" % j, None)
            if all((o, j) in crosses for o in range(REACH + 1)):
                for name in ("own", "rows", "r1", "r2", "r3", "r4"):
                    keep.pop("%s/%d" % (name, j), None)
        keep.update(made)
        held = lax.optimization_barrier(keep)

    out = held.get("out")
    if out is None:
        out = jnp.zeros((SLOTS, width, LAGS, stations), jnp.bfloat16)
    for o in range(REACH + 1):
        if o not in lag_done:
            out = lag_into(out, o, held["cross%d" % o])
    return out[None]


def solution(mesh):
    staged = mesh.shape["blk"] == 8
    placed = (P("blk", "freq", None, None, None), P("blk", None), P("blk"))
    return jax.shard_map(
        lambda s, po, pc: local(s, po, pc, staged),
        mesh=mesh,
        in_specs=placed,
        out_specs=P("blk", None, "freq", None, None),
        check_vma=False,
    )
```

```python
import math

import jax
import jax.numpy as jnp
import numpy as np
from jax import lax
from jax.sharding import PartitionSpec as P

F = 512
LAGS = 256
REACH = 4
SLOTS = 5
CHUNKS = 8


def from_behind(shard, axis, by):
    size = lax.axis_size(axis)
    return lax.ppermute(shard, axis, [(i, (i + by) % size) for i in range(size)])


def swap(shard, axis, mask):
    size = lax.axis_size(axis)
    return lax.ppermute(shard, axis, [(i, i ^ mask) for i in range(size)])


def lag_table(bins_order):
    shifted = jnp.arange(LAGS, dtype=jnp.int32) - LAGS // 2
    bins = jnp.asarray(bins_order, dtype=jnp.int32) + 1
    phase = jnp.mod(shifted[:, None] * bins[None, :], 2 * F).astype(jnp.float32) * (jnp.pi / F)
    return jnp.stack([jnp.cos(phase), -jnp.sin(phase)], axis=-1).astype(jnp.bfloat16)


def home_rows(own, start, width):
    freq_count, parts_count, windows, stations = own.shape
    flat = own.reshape(freq_count, parts_count * windows, stations)
    picked = lax.dynamic_slice_in_dim(jnp.transpose(flat, (0, 2, 1)), start, width, axis=1)
    turned = jnp.concatenate([-picked[..., windows:], picked[..., :windows]], axis=2)
    return jnp.concatenate([picked, turned], axis=1)


def cross_spectrum(rows_t, partner):
    freq_count, parts_count, windows, stations = partner.shape
    width = rows_t.shape[1] // 2
    columns = partner.reshape(freq_count, parts_count * windows, stations)
    summed = jnp.einsum("fSk,fkt->fSt", rows_t, columns, preferred_element_type=jnp.float32)
    return (summed / windows).astype(jnp.bfloat16).reshape(freq_count, 2, width, stations)


def local(spectra, pair_offsets, pair_count, staged):
    own_part = spectra[0]
    local_freqs, _, _, stations = own_part.shape
    parts = lax.axis_size("freq")
    freq_total = local_freqs * parts
    chunks = CHUNKS if local_freqs % CHUNKS == 0 else 1
    piece = local_freqs // chunks
    width = stations // parts
    q = lax.axis_index("freq")
    b = lax.axis_index("blk")
    x_bit = (b // 2) % 2
    core = b % 2

    order = np.array(
        [qq * local_freqs + j * piece + i for j in range(chunks) for qq in range(parts) for i in range(piece)]
    )
    held = {"part/%d" % j: own_part[j * piece:(j + 1) * piece] for j in range(chunks)}
    crosses = {}
    depth = 4 if staged else 1
    for step in range(chunks + depth + 1):
        made = {}
        j = step
        if j < chunks:
            made["own/%d" % j] = lax.all_gather(held["part/%d" % j], "freq", axis=0, tiled=True)
        j = step - 1
        if 0 <= j < chunks:
            own = held["own/%d" % j]
            made["rows/%d" % j] = home_rows(own, q * width, width)
            part = cross_spectrum(made["rows/%d" % j], own)
            base = held.get("cross0")
            if base is None:
                base = jnp.zeros((freq_total, 2, width, stations), jnp.bfloat16)
            made["cross0"] = lax.dynamic_update_slice(base, part, (j * piece * parts, 0, 0, 0))
            crosses[(0, j)] = True
            if staged:
                made["r4/%d" % j] = swap(own, "blk", 4)
            else:
                for o in range(1, REACH + 1):
                    made["r%d/%d" % (o, j)] = from_behind(own, "blk", -o)
        if staged:
            j = step - 2
            if 0 <= j < chunks:
                made["r2/%d" % j] = swap(jnp.where(x_bit == 1, held["own/%d" % j], held["r4/%d" % j]), "blk", 2)
            j = step - 3
            if 0 <= j < chunks:
                made["r1/%d" % j] = swap(jnp.where(core == 1, held["own/%d" % j], held["r2/%d" % j]), "blk", 1)
                made["r3/%d" % j] = swap(jnp.where(core == 1, held["r2/%d" % j], held["r4/%d" % j]), "blk", 1)
        for key in list(held):
            if "/" not in key:
                continue
            name, j = key.split("/")[0], int(key.split("/")[-1])
            if name in ("own", "r1", "r2", "r3", "r4"):
                o = 0 if name == "own" else int(name[1])
                if "rows/%d" % j in held and (o, j) not in crosses:
                    part = cross_spectrum(held["rows/%d" % j], held[key])
                    name = "cross%d" % o
                    base = made.get(name, held.get(name))
                    if base is None:
                        base = jnp.zeros((freq_total, 2, width, stations), jnp.bfloat16)
                    made[name] = lax.dynamic_update_slice(base, part, (j * piece * parts, 0, 0, 0))
                    crosses[(o, j)] = True
        keep = dict(held)
        for j in range(chunks):
            if step >= j:
                keep.pop("part/%d" % j, None)
            if all((o, j) in crosses for o in range(REACH + 1)):
                for name in ("own", "rows", "r1", "r2", "r3", "r4"):
                    keep.pop("%s/%d" % (name, j), None)
        keep.update(made)
        held = lax.optimization_barrier(keep)

    offsets = pair_offsets[0]
    listed = pair_count[0]
    weights = lag_table(order).reshape(LAGS, freq_total * 2)
    scale = math.sqrt(2.0 / freq_total)
    out = jnp.zeros((SLOTS, width, LAGS, stations), jnp.bfloat16)
    for o in range(REACH + 1):
        slot = jnp.argmax(offsets == o).astype(jnp.int32)
        cross = held["cross%d" % o].reshape(freq_total * 2, width, stations)
        lagged = jnp.einsum("lK,Kst->lst", weights, cross, preferred_element_type=jnp.float32)
        factor = jnp.where(slot < listed, scale, 0.0).astype(jnp.float32)
        result = jnp.transpose((lagged * factor).astype(jnp.bfloat16), (1, 0, 2))
        out = lax.dynamic_update_slice(out, result[None], (slot, 0, 0, 0))
    return out[None]


def solution(mesh):
    staged = mesh.shape["blk"] == 8
    placed = (P("blk", "freq", None, None, None), P("blk", None), P("blk"))
    return jax.shard_map(
        lambda s, po, pc: local(s, po, pc, staged),
        mesh=mesh,
        in_specs=placed,
        out_specs=P("blk", None, "freq", None, None),
        check_vma=False,
    )
```
